32 devices in a mesh: blk: 16 (over z, y, core), rep: 2 (over x).
Axes of the slice: x: 2, y: 2, z: 4, core: 2. Of those that a mesh axis runs over, the one named last changes fastest.
Arguments:
- qm_pos: float32 [3, 2048], P(None, 'blk'), may hold values from -4 to 4
- species: int32 [2048], P('blk'), may hold values from 0 to 7
- qm_count: int32 [16], P('blk'), may hold values from 64 to 128, as said below
- ghost_owner: int32 [2048, 4], P('blk'), may hold values from 0 to 15, all different within a row; in each aligned block of 128 rows (0 to 127, 128 to 255, ...) at most 64 rows name the same one
- ghost_slot: int32 [2048, 4], P('blk'), may hold values from 0 to 127
- mm_pos: float32 [3, 16384], P(None, ('blk', 'rep')), may hold values from -4 to 4
- mm_charge: float32 [16384], P(('blk', 'rep')), may hold values from -6 to 6
- species_table: bfloat16 [8, 128], replicated, may hold values from -6 to 6
- potential_gain: float32 [128], replicated, may hold values from -8 to 8
- message_weight: bfloat16 [128, 128], replicated, may hold values from -0.25 to 0.25
- hidden_weight: bfloat16 [128, 256], replicated, may hold values from -0.5 to 0.5
- energy_readout: float32 [256], replicated, may hold values from -0.375 to 0.375
- charge_readout: float32 [256], replicated, may hold values from -0.375 to 0.375
Outputs:
- atom_energy: float32 [2048], P('blk')
- qm_force: float32 [3, 2048], P(None, 'blk')
- mm_force: float32 [3, 16384], P(None, ('blk', 'rep'))
The draws below stay inside these ranges and needn't reach their ends.
Inputs may be any that keep to these rules, and one draw needn't show every extreme that they name: `qm_count`: some block holds exactly 128 live atoms. `ghost_owner`: each row names 4 different blocks; among the rows of one device no block is named more than 64 times, and some block exactly 64 times.
All inputs are finite; a program needn't handle non-finite values.
Results may differ from the reference program's by a relative error of at most 0.0055.
Values may be sent and summed in bfloat16 or wider, within the bound.
No kernel may reach another device: no remote copies, remote signals or barrier semaphores. Data moves between devices by JAX's collectives and lax.ppermute only.
A program may use at most 64 MiB of HBM per device.

```python
import math
import jax
import jax.numpy as jnp
import numpy as np
from jax import lax

A_DEV = 128
F = 128
H = 256
S = 8
K = 4
NQM = 2048
NMM = 16384
CAP = 64
N_BLK = 16


def draw_qm_count(key, part):
    key_counts, key_full = jax.random.split(key)
    counts = jax.random.randint(key_counts, (N_BLK,), A_DEV // 2, A_DEV + 1)
    chosen = jax.random.randint(key_full, (), 0, N_BLK)
    return jnp.where(jnp.arange(N_BLK) == chosen, A_DEV, counts).astype(jnp.int32)


def plant(result, rng, least, high):
    longest = result.shape.index(max(result.shape))
    spots = []
    for shift in (0, 1):
        where = [jax.random.randint(jax.random.fold_in(rng, axis), (), 0, length) for axis, length in enumerate(result.shape)]
        where[longest] = (where[longest] + shift) % result.shape[longest]
        spots.append(tuple(where))
    return result.at[spots[0]].set(least).at[spots[1]].set(high)


def level_of(stream_key, dims, shards, low, high):
    loudness, own = 1.0, jax.random.fold_in(stream_key, 6)
    for position, shards_of in shards:
        draws = jnp.exp(jax.random.uniform(jax.random.fold_in(own, position), (shards_of,), jnp.float32, low / len(shards), high / len(shards)))
        loudness = loudness * jnp.repeat(draws, dims[position] // shards_of).reshape([-1 if axis == position else 1 for axis in range(len(dims))])
    return loudness


def routed_block(stream_key, own, number, rows, number_of, top, limit, lean):
    ranking = jax.random.permutation(stream_key, number_of)
    crowded, common = load_shares(number_of, rows * top, limit, lean, True), load_shares(number_of, rows * top, limit, lean, False)
    places = jnp.arange(number_of)

    def named(sizes, offset_by):
        used = int((sizes > 0).sum())
        fixed = max(1, used // 4)
        passed = fixed + (places - fixed + offset_by * (used - fixed)) % max(1, number_of - fixed)
        return jnp.zeros((number_of,), jnp.int32).at[ranking[jnp.where(places < fixed, places, passed)]].set(jnp.asarray(sizes, jnp.int32))

    sizes = jnp.where(number % 4 == 0, named(crowded, number // 4), named(common, number - number // 4 - 1))
    mixed = jax.random.permutation(jax.random.fold_in(own, 3), number_of)
    giver, receiver = mixed[0:number_of // 2 * 2:2], mixed[1:number_of // 2 * 2:2]
    margin = jnp.minimum(sizes[giver] - 1, limit - sizes[receiver]) // 2
    margin = jnp.where((giver == ranking[0]) | (receiver == ranking[0]) | (sizes[receiver] == 0), 0, jnp.maximum(margin, 0))
    passed = jax.random.randint(jax.random.fold_in(own, 4), (number_of // 2,), 0, 1 << 20) % (margin + 1)
    sizes = sizes.at[giver].add(-passed).at[receiver].add(passed)
    items = jnp.searchsorted(jnp.cumsum(sizes), jnp.arange(rows * top), side="right").astype(jnp.int32)
    listing = items.reshape(top, rows).T
    listing = listing[jax.random.permutation(jax.random.fold_in(own, 1), rows)]
    offset_by = jax.random.randint(jax.random.fold_in(own, 2), (rows, 1), 0, top)
    return jnp.take_along_axis(listing, (jnp.arange(top)[None, :] + offset_by) % top, axis=1)


def load_shares(number_of, total, bound, lean, full):
    portions = [(1 << 20) // math.isqrt(grade ** lean) + 1 for grade in range(1, number_of + 1)]
    largest = bound if full else min(bound, max(-(-total // number_of), total * portions[0] // sum(portions)))
    least = 1 if total - largest >= number_of - 1 else 0
    given, surplus = [largest] + [least] * (number_of - 1), total - largest - least * (number_of - 1)
    while surplus > 0:
        movable = [i for i in range(1, number_of) if given[i] < largest] or [i for i in range(1, number_of) if given[i] < bound]
        pool, remaining = sum([portions[i] for i in movable]), surplus
        for i in movable:
            addition = min(bound - given[i], max(1, remaining * portions[i] // pool), surplus)
            given[i] = given[i] + addition
            surplus = surplus - addition
    return np.array(given)


def noise(rng, extent, scale, reach, pieces=(), kind=jnp.bfloat16):
    result = jax.random.normal(rng, extent, jnp.float32) * scale
    if len(pieces) > 0:
        result = level_of(rng, extent, pieces, -0.22, 0.18) * result
    return jnp.clip(result, min=-reach, max=reach).astype(kind)


def setup_inputs(seed: int = 0) -> dict:
    streams_of = jax.random.split(jax.random.key(seed), 14)
    qm_pos = jnp.clip(jax.random.uniform(streams_of[0], (3, NQM), jnp.float32, -4.0, 4.0) * level_of(streams_of[0], (3, NQM), ((1, 16),), -0.4, 0.0), -4.0, 4.0)
    species = plant(jax.random.randint(streams_of[1], (NQM,), 0, S), jax.random.fold_in(streams_of[1], 1), 0, S - 1).astype(jnp.int32)
    qm_count = draw_qm_count(jax.random.fold_in(streams_of[13], 71), 0)
    ghost_owner_keys = jax.random.split(jax.random.fold_in(streams_of[3], 1), NQM // A_DEV)
    ghost_owner_turns = jax.random.permutation(jax.random.fold_in(streams_of[3], 3), NQM // A_DEV)
    ghost_owner = jax.vmap(lambda own, number: routed_block(jax.random.fold_in(streams_of[3], 2), own, number, A_DEV, N_BLK, K, CAP, 2))(ghost_owner_keys, ghost_owner_turns).reshape((NQM, K))
    ghost_slot = plant(jax.random.randint(streams_of[4], (NQM, K), 0, A_DEV), jax.random.fold_in(streams_of[4], 1), 0, A_DEV - 1).astype(jnp.int32)
    mm_pos = jnp.clip(jax.random.uniform(streams_of[5], (3, NMM), jnp.float32, -4.0, 4.0) * level_of(streams_of[5], (3, NMM), ((1, 32),), -0.4, 0.0), -4.0, 4.0)
    mm_charge = noise(streams_of[6], (NMM,), 1.0, 6.0, ((0, 32),), jnp.float32)
    species_table = noise(streams_of[7], (S, F), 1.0, 6.0)
    potential_gain = noise(streams_of[8], (F,), 2.0, 8.0, (), jnp.float32)
    message_weight = noise(streams_of[9], (F, F), (K * F) ** -0.5, 0.25)
    hidden_weight = noise(streams_of[10], (F, H), F ** -0.5, 0.5)
    energy_readout = noise(streams_of[11], (H,), H ** -0.5, 0.375, (), jnp.float32)
    charge_readout = noise(streams_of[12], (H,), H ** -0.5, 0.375, (), jnp.float32)
    return {"qm_pos": qm_pos, "species": species, "qm_count": qm_count, "ghost_owner": ghost_owner, "ghost_slot": ghost_slot, "mm_pos": mm_pos, "mm_charge": mm_charge, "species_table": species_table, "potential_gain": potential_gain, "message_weight": message_weight, "hidden_weight": hidden_weight, "energy_readout": energy_readout, "charge_readout": charge_readout}


SOFTEN = 0.25

def reference(qm_pos, species, qm_count, ghost_owner, ghost_slot, mm_pos, mm_charge, species_table, potential_gain, message_weight, hidden_weight, energy_readout, charge_readout):
    coupling = float(NMM) ** (-0.5)
    qm_groups = jnp.transpose(qm_pos.reshape(3, N_BLK, A_DEV), (1, 0, 2))

    def potential_block(places):
        offset = places[:, :, None] - mm_pos[:, None, :]
        inverse = lax.rsqrt(lax.optimization_barrier(jnp.sum(offset * offset, axis=0)) + SOFTEN)
        return lax.optimization_barrier(jnp.sum(inverse * mm_charge[None, :], axis=1))
    potential = lax.map(potential_block, qm_groups).reshape(NQM) * coupling
    live = (jnp.arange(A_DEV)[None, :] < qm_count[:, None]).reshape(NQM).astype(jnp.float32)
    picks = (species[:, None] == jnp.arange(S)[None, :]).astype(jnp.bfloat16)
    base = jnp.dot(picks, species_table, preferred_element_type=jnp.float32)
    start = (live[:, None] * (base + potential[:, None] * potential_gain[None, :])).astype(jnp.bfloat16)
    ghost_index = (ghost_owner * A_DEV + ghost_slot).astype(jnp.int32)
    ghosts = jnp.take(start, ghost_index.reshape(-1), axis=0).astype(jnp.float32)
    neighbour = lax.optimization_barrier(jnp.sum(ghosts.reshape(NQM, K, F), axis=1)).astype(jnp.bfloat16)
    mixed = start.astype(jnp.float32) + jnp.dot(neighbour, message_weight, preferred_element_type=jnp.float32)
    mixed_b = mixed.astype(jnp.bfloat16)
    before = jnp.dot(mixed_b, hidden_weight, preferred_element_type=jnp.float32)
    sigma = jax.nn.sigmoid(before)
    active = before * sigma
    energy_part = live * lax.optimization_barrier(jnp.sum(active * energy_readout[None, :], axis=1))
    charge_part = live * lax.optimization_barrier(jnp.sum(active * charge_readout[None, :], axis=1))
    atom_energy = energy_part + charge_part * potential
    back_active = live[:, None] * (energy_readout[None, :] + potential[:, None] * charge_readout[None, :])
    back_before = (back_active * sigma * (1.0 + before * (1.0 - sigma))).astype(jnp.bfloat16)
    back_mixed = jnp.dot(back_before, hidden_weight.T, preferred_element_type=jnp.float32)
    back_sum = jnp.dot(back_mixed.astype(jnp.bfloat16), message_weight.T, preferred_element_type=jnp.float32).astype(jnp.bfloat16)
    spread = jnp.repeat(back_sum.astype(jnp.float32), K, axis=0)
    back_start = back_mixed + jnp.zeros((NQM, F), jnp.float32).at[ghost_index.reshape(-1)].add(spread)
    effective = charge_part + live * lax.optimization_barrier(jnp.sum(back_start * potential_gain[None, :], axis=1))
    stacked = jnp.concatenate([qm_groups, effective.reshape(N_BLK, 1, A_DEV)], axis=1)

    def force_block(mm_running, group):
        offset = group[:3, :, None] - mm_pos[:, None, :]
        inverse = lax.rsqrt(lax.optimization_barrier(jnp.sum(offset * offset, axis=0)) + SOFTEN)
        weight = inverse * inverse * inverse * mm_charge[None, :]
        pull = lax.optimization_barrier(jnp.sum(offset * weight[None], axis=2)) * group[3][None, :]
        mm_running = mm_running - lax.optimization_barrier(jnp.sum(offset * (weight * group[3][:, None])[None], axis=1))
        return (mm_running, pull)
    mm_sum, pulls = lax.scan(force_block, jnp.zeros((3, NMM), jnp.float32), stacked)
    qm_force = jnp.transpose(pulls, (1, 0, 2)).reshape(3, NQM) * coupling
    return (atom_energy, qm_force, mm_sum * coupling)
```

```python
import jax
import jax.numpy as jnp
from jax import lax
from jax.sharding import PartitionSpec as P

SOFTEN = 0.25
CHUNK = 512


def gather_doubling(x, axis):
    n = lax.axis_size(axis)
    me = lax.axis_index(axis)
    step = 1
    while step < n:
        other = lax.ppermute(x, axis, [(i, i ^ step) for i in range(n)])
        low = (me // step) % 2 == 0
        x = jnp.where(low, jnp.concatenate([x, other], -1), jnp.concatenate([other, x], -1))
        step *= 2
    return x


def sum_butterfly(x, axis):
    n = lax.axis_size(axis)
    step = 1
    while step < n:
        x = x + lax.ppermute(x, axis, [(i, i ^ step) for i in range(n)])
        step *= 2
    return x


def potential_pass(qm_all, mm_pos, mm_charge):
    mm_col = [mm_pos[c][:, None] for c in range(3)]
    q_col = mm_charge[:, None]
    chunks = qm_all.shape[1] // CHUNK

    def body(block):
        d = [block[c][None, :] - mm_col[c] for c in range(3)]
        inverse = lax.rsqrt(d[0] * d[0] + d[1] * d[1] + d[2] * d[2] + SOFTEN)
        weighted = inverse * q_col
        cubed = weighted * inverse * inverse
        return jnp.stack(
            [jnp.sum(weighted, axis=0)] + [jnp.sum(d[c] * cubed, axis=0) for c in range(3)]
        )

    parts = lax.map(body, jnp.transpose(qm_all.reshape(3, chunks, CHUNK), (1, 0, 2)))
    return jnp.transpose(parts, (1, 0, 2)).reshape(4, qm_all.shape[1])


def force_pass(qm_all, effective, mm_pos):
    chunks = qm_all.shape[1] // CHUNK
    stacked = jnp.concatenate([qm_all, effective[None, :]], axis=0)
    stacked = jnp.transpose(stacked.reshape(4, chunks, CHUNK), (1, 2, 0))

    def body(running, block):
        d = [block[:, c : c + 1] - mm_pos[c][None, :] for c in range(3)]
        inverse = lax.rsqrt(d[0] * d[0] + d[1] * d[1] + d[2] * d[2] + SOFTEN)
        weight = inverse * inverse * inverse * block[:, 3:4]
        return running + jnp.stack([jnp.sum(d[c] * weight, axis=0) for c in range(3)]), None

    total, _ = lax.scan(body, jnp.zeros((3, mm_pos.shape[1]), jnp.float32), stacked)
    return total


def on_device(
    qm_pos,
    species,
    qm_count,
    ghost_owner,
    ghost_slot,
    mm_pos,
    mm_charge,
    species_table,
    potential_gain,
    message_weight,
    hidden_weight,
    energy_readout,
    charge_readout,
):
    rows = qm_pos.shape[1]
    blocks = lax.axis_size("blk")
    me = lax.axis_index("blk")
    kinds = species_table.shape[0]
    coupling = float(mm_pos.shape[1] * blocks * lax.axis_size("rep")) ** (-0.5)

    own = jnp.concatenate(
        [
            qm_pos,
            species.astype(jnp.float32)[None, :],
            jnp.broadcast_to(qm_count.astype(jnp.float32)[None, :], (1, rows)),
        ],
        axis=0,
    )
    known = gather_doubling(own, "blk")
    qm_all = known[:3]
    atoms = qm_all.shape[1]
    species_all = known[3].astype(jnp.int32)
    live_all = ((jnp.arange(atoms) % rows).astype(jnp.float32) < known[4]).astype(jnp.float32)

    partial = potential_pass(qm_all, mm_pos, mm_charge)
    total = sum_butterfly(sum_butterfly(partial, "rep"), "blk")
    potential_all = total[0] * coupling
    pull = lax.dynamic_slice_in_dim(total[1:4], me * rows, rows, axis=1)

    picks_all = (species_all[:, None] == jnp.arange(kinds)[None, :]).astype(jnp.bfloat16)
    base_all = jnp.dot(picks_all, species_table, preferred_element_type=jnp.float32)
    start_all = (
        live_all[:, None] * (base_all + potential_all[:, None] * potential_gain[None, :])
    ).astype(jnp.bfloat16)
    live = lax.dynamic_slice_in_dim(live_all, me * rows, rows)
    potential = lax.dynamic_slice_in_dim(potential_all, me * rows, rows)
    start = lax.dynamic_slice_in_dim(start_all, me * rows, rows, axis=0)

    ghost = ghost_owner * rows + ghost_slot
    columns = jnp.arange(atoms)[None, :]
    links = jnp.zeros((rows, atoms), jnp.bfloat16)
    for k in range(ghost.shape[1]):
        links = links + (ghost[:, k : k + 1] == columns).astype(jnp.bfloat16)
    neighbour = jnp.dot(links, start_all, preferred_element_type=jnp.float32).astype(jnp.bfloat16)

    mixed = start.astype(jnp.float32) + jnp.dot(
        neighbour, message_weight, preferred_element_type=jnp.float32
    )
    before = jnp.dot(mixed.astype(jnp.bfloat16), hidden_weight, preferred_element_type=jnp.float32)
    sigma = jax.nn.sigmoid(before)
    active = before * sigma
    energy_part = live * jnp.sum(active * energy_readout[None, :], axis=1)
    charge_part = live * jnp.sum(active * charge_readout[None, :], axis=1)
    atom_energy = energy_part + charge_part * potential
    back_active = live[:, None] * (
        energy_readout[None, :] + potential[:, None] * charge_readout[None, :]
    )
    back_before = (back_active * sigma * (1.0 + before * (1.0 - sigma))).astype(jnp.bfloat16)
    back_mixed = jnp.dot(back_before, hidden_weight.T, preferred_element_type=jnp.float32)
    back_sum = jnp.dot(
        back_mixed.astype(jnp.bfloat16), message_weight.T, preferred_element_type=jnp.float32
    ).astype(jnp.bfloat16)

    sent = jnp.sum(back_sum.astype(jnp.float32) * potential_gain[None, :], axis=1)
    spread = jnp.sum(links.astype(jnp.float32) * sent[:, None], axis=0) * live_all
    local = charge_part + live * jnp.sum(back_mixed * potential_gain[None, :], axis=1)
    placed = (jnp.arange(atoms) // rows == me).astype(jnp.float32)
    local_all = jnp.tile(local, atoms // rows) * placed
    effective_all = sum_butterfly(spread + local_all, "blk")
    effective = lax.dynamic_slice_in_dim(effective_all, me * rows, rows)

    qm_force = pull * (effective * coupling)[None, :]
    mm_force = force_pass(qm_all, effective_all, mm_pos) * (-coupling * mm_charge)[None, :]
    return (atom_energy, qm_force, mm_force)


def solution(mesh):
    placed = (
        P(None, "blk"),
        P("blk"),
        P("blk"),
        P("blk", None),
        P("blk", None),
        P(None, ("blk", "rep")),
        P(("blk", "rep")),
        P(),
        P(),
        P(),
        P(),
        P(),
        P(),
    )
    return jax.shard_map(
        on_device,
        mesh=mesh,
        in_specs=placed,
        out_specs=(P("blk"), P(None, "blk"), P(None, ("blk", "rep"))),
        check_vma=False,
    )
```

```python
import jax
import jax.numpy as jnp
from jax import lax
from jax.sharding import PartitionSpec as P

SOFTEN = 0.25
CHUNK = 512


def gather_doubling(x, axis, first=1, last=None):
    n = lax.axis_size(axis)
    last = n if last is None else last
    me = lax.axis_index(axis)
    step = first
    while step < last:
        other = lax.ppermute(x, axis, [(i, i ^ step) for i in range(n)])
        low = (me // step) % 2 == 0
        x = jnp.where(low, jnp.concatenate([x, other], -1), jnp.concatenate([other, x], -1))
        step *= 2
    return x


def sum_butterfly(x, axis, last=None):
    n = lax.axis_size(axis)
    last = n if last is None else last
    step = 1
    while step < last:
        x = x + lax.ppermute(x, axis, [(i, i ^ step) for i in range(n)])
        step *= 2
    return x


def potential_pass(qm_some, mm_some):
    chunks = mm_some.shape[1] // CHUNK
    cols = [qm_some[c][None, :] for c in range(3)]

    def body(running, block):
        d = [cols[c] - block[:, c : c + 1] for c in range(3)]
        inverse = lax.rsqrt(d[0] * d[0] + d[1] * d[1] + d[2] * d[2] + SOFTEN)
        weighted = inverse * block[:, 3:4]
        cubed = weighted * inverse * inverse
        part = jnp.stack(
            [jnp.sum(weighted, axis=0)] + [jnp.sum(d[c] * cubed, axis=0) for c in range(3)]
        )
        return running + part, None

    stacked = jnp.transpose(mm_some.reshape(4, chunks, CHUNK), (1, 2, 0))
    total, _ = lax.scan(body, jnp.zeros((4, qm_some.shape[1]), jnp.float32), stacked)
    return total


def force_pass(qm_all, effective, mm_pos):
    chunks = qm_all.shape[1] // CHUNK
    stacked = jnp.concatenate([qm_all, effective[None, :]], axis=0)
    stacked = jnp.transpose(stacked.reshape(4, chunks, CHUNK), (1, 2, 0))

    def body(running, block):
        d = [block[:, c : c + 1] - mm_pos[c][None, :] for c in range(3)]
        inverse = lax.rsqrt(d[0] * d[0] + d[1] * d[1] + d[2] * d[2] + SOFTEN)
        weight = inverse * inverse * inverse * block[:, 3:4]
        return running + jnp.stack([jnp.sum(d[c] * weight, axis=0) for c in range(3)]), None

    total, _ = lax.scan(body, jnp.zeros((3, mm_pos.shape[1]), jnp.float32), stacked)
    return total


def on_device(
    qm_pos,
    species,
    qm_count,
    ghost_owner,
    ghost_slot,
    mm_pos,
    mm_charge,
    species_table,
    potential_gain,
    message_weight,
    hidden_weight,
    energy_readout,
    charge_readout,
):
    rows = qm_pos.shape[1]
    blocks = lax.axis_size("blk")
    me = lax.axis_index("blk")
    kinds = species_table.shape[0]
    coupling = float(mm_pos.shape[1] * blocks * lax.axis_size("rep")) ** (-0.5)

    low_blocks = 1
    while low_blocks * low_blocks < blocks:
        low_blocks *= 2
    own = jnp.concatenate(
        [
            qm_pos,
            species.astype(jnp.float32)[None, :],
            jnp.broadcast_to(qm_count.astype(jnp.float32)[None, :], (1, rows)),
        ],
        axis=0,
    )
    near = gather_doubling(own, "blk", 1, low_blocks)
    mm_some = gather_doubling(
        jnp.concatenate([mm_pos, mm_charge[None, :]], axis=0), "blk", low_blocks, blocks
    )
    partial = potential_pass(near[:3], mm_some)
    total = sum_butterfly(sum_butterfly(partial, "rep"), "blk", low_blocks)
    pull = lax.dynamic_slice_in_dim(total[1:4], (me % low_blocks) * rows, rows, axis=1)
    known = gather_doubling(
        jnp.concatenate([total[0:1] * coupling, near], axis=0), "blk", low_blocks, blocks
    )
    potential_all = known[0]
    qm_all = known[1:4]
    atoms = qm_all.shape[1]
    species_all = known[4].astype(jnp.int32)
    live_all = ((jnp.arange(atoms) % rows).astype(jnp.float32) < known[5]).astype(jnp.float32)

    picks_all = (species_all[:, None] == jnp.arange(kinds)[None, :]).astype(jnp.bfloat16)
    base_all = jnp.dot(picks_all, species_table, preferred_element_type=jnp.float32)
    start_all = (
        live_all[:, None] * (base_all + potential_all[:, None] * potential_gain[None, :])
    ).astype(jnp.bfloat16)
    live = lax.dynamic_slice_in_dim(live_all, me * rows, rows)
    potential = lax.dynamic_slice_in_dim(potential_all, me * rows, rows)
    start = lax.dynamic_slice_in_dim(start_all, me * rows, rows, axis=0)

    ghost = ghost_owner * rows + ghost_slot
    columns = jnp.arange(atoms)[None, :]
    links = jnp.zeros((rows, atoms), jnp.bfloat16)
    for k in range(ghost.shape[1]):
        links = links + (ghost[:, k : k + 1] == columns).astype(jnp.bfloat16)
    neighbour = jnp.dot(links, start_all, preferred_element_type=jnp.float32).astype(jnp.bfloat16)

    mixed = start.astype(jnp.float32) + jnp.dot(
        neighbour, message_weight, preferred_element_type=jnp.float32
    )
    before = jnp.dot(mixed.astype(jnp.bfloat16), hidden_weight, preferred_element_type=jnp.float32)
    sigma = jax.nn.sigmoid(before)
    active = before * sigma
    energy_part = live * jnp.sum(active * energy_readout[None, :], axis=1)
    charge_part = live * jnp.sum(active * charge_readout[None, :], axis=1)
    atom_energy = energy_part + charge_part * potential
    back_active = live[:, None] * (
        energy_readout[None, :] + potential[:, None] * charge_readout[None, :]
    )
    back_before = (back_active * sigma * (1.0 + before * (1.0 - sigma))).astype(jnp.bfloat16)
    back_mixed = jnp.dot(back_before, hidden_weight.T, preferred_element_type=jnp.float32)
    back_sum = jnp.dot(
        back_mixed.astype(jnp.bfloat16), message_weight.T, preferred_element_type=jnp.float32
    ).astype(jnp.bfloat16)

    sent = jnp.sum(back_sum.astype(jnp.float32) * potential_gain[None, :], axis=1)
    spread = jnp.sum(links.astype(jnp.float32) * sent[:, None], axis=0) * live_all
    local = charge_part + live * jnp.sum(back_mixed * potential_gain[None, :], axis=1)
    placed = (jnp.arange(atoms) // rows == me).astype(jnp.float32)
    local_all = jnp.tile(local, atoms // rows) * placed
    effective_all = sum_butterfly(spread + local_all, "blk")
    effective = lax.dynamic_slice_in_dim(effective_all, me * rows, rows)

    qm_force = pull * (effective * coupling)[None, :]
    mm_force = force_pass(qm_all, effective_all, mm_pos) * (-coupling * mm_charge)[None, :]
    return (atom_energy, qm_force, mm_force)


def solution(mesh):
    placed = (
        P(None, "blk"),
        P("blk"),
        P("blk"),
        P("blk", None),
        P("blk", None),
        P(None, ("blk", "rep")),
        P(("blk", "rep")),
        P(),
        P(),
        P(),
        P(),
        P(),
        P(),
    )
    return jax.shard_map(
        on_device,
        mesh=mesh,
        in_specs=placed,
        out_specs=(P("blk"), P(None, "blk"), P(None, ("blk", "rep"))),
        check_vma=False,
    )
```

```python
import jax
import jax.numpy as jnp
from jax import lax
from jax.sharding import PartitionSpec as P

SOFTEN = 0.25
CHUNK = 512


def gather_doubling(x, axis, first=1, last=None):
    n = lax.axis_size(axis)
    last = n if last is None else last
    me = lax.axis_index(axis)
    step = first
    while step < last:
        other = lax.ppermute(x, axis, [(i, i ^ step) for i in range(n)])
        low = (me // step) % 2 == 0
        x = jnp.where(low, jnp.concatenate([x, other], -1), jnp.concatenate([other, x], -1))
        step *= 2
    return x


def sum_butterfly(x, axis, last=None):
    n = lax.axis_size(axis)
    last = n if last is None else last
    step = 1
    while step < last:
        x = x + lax.ppermute(x, axis, [(i, i ^ step) for i in range(n)])
        step *= 2
    return x


def potential_pass(qm_some, mm_some):
    chunks = mm_some.shape[1] // CHUNK
    cols = [qm_some[c][None, :] for c in range(3)]

    def body(running, block):
        d = [cols[c] - block[:, c : c + 1] for c in range(3)]
        inverse = lax.rsqrt(d[0] * d[0] + d[1] * d[1] + d[2] * d[2] + SOFTEN)
        weighted = inverse * block[:, 3:4]
        cubed = weighted * inverse * inverse
        part = jnp.stack(
            [jnp.sum(weighted, axis=0)] + [jnp.sum(d[c] * cubed, axis=0) for c in range(3)]
        )
        return running + part, None

    stacked = jnp.transpose(mm_some.reshape(4, chunks, CHUNK), (1, 2, 0))
    total, _ = lax.scan(body, jnp.zeros((4, qm_some.shape[1]), jnp.float32), stacked)
    return total


def force_geometry(qm_all, mm_pos):
    chunks = qm_all.shape[1] // CHUNK
    stacked = jnp.transpose(qm_all.reshape(3, chunks, CHUNK), (1, 2, 0))

    def body(block):
        d = [block[:, c : c + 1] - mm_pos[c][None, :] for c in range(3)]
        inverse = lax.rsqrt(d[0] * d[0] + d[1] * d[1] + d[2] * d[2] + SOFTEN)
        return inverse * inverse * inverse

    return lax.map(body, stacked)


def force_pass(qm_all, effective, mm_pos, cubes):
    chunks = qm_all.shape[1] // CHUNK
    stacked = jnp.concatenate([qm_all, effective[None, :]], axis=0)
    stacked = jnp.transpose(stacked.reshape(4, chunks, CHUNK), (1, 2, 0))

    def body(running, item):
        block, cube = item
        weight = cube * block[:, 3:4]
        d = [block[:, c : c + 1] - mm_pos[c][None, :] for c in range(3)]
        return running + jnp.stack([jnp.sum(d[c] * weight, axis=0) for c in range(3)]), None

    total, _ = lax.scan(body, jnp.zeros((3, mm_pos.shape[1]), jnp.float32), (stacked, cubes))
    return total


def on_device(
    qm_pos,
    species,
    qm_count,
    ghost_owner,
    ghost_slot,
    mm_pos,
    mm_charge,
    species_table,
    potential_gain,
    message_weight,
    hidden_weight,
    energy_readout,
    charge_readout,
):
    rows = qm_pos.shape[1]
    blocks = lax.axis_size("blk")
    me = lax.axis_index("blk")
    kinds = species_table.shape[0]
    coupling = float(mm_pos.shape[1] * blocks * lax.axis_size("rep")) ** (-0.5)

    low_blocks = 1
    while low_blocks * low_blocks < blocks:
        low_blocks *= 2
    own = jnp.concatenate(
        [
            qm_pos,
            species.astype(jnp.float32)[None, :],
            jnp.broadcast_to(qm_count.astype(jnp.float32)[None, :], (1, rows)),
        ],
        axis=0,
    )
    near = gather_doubling(own, "blk", 1, low_blocks)
    mm_some = jnp.concatenate([mm_pos, mm_charge[None, :]], axis=0)
    partial = potential_pass(near[:3], mm_some)
    step = low_blocks
    while step < blocks:
        other = lax.ppermute(mm_some, "blk", [(i, i ^ step) for i in range(blocks)])
        partial = partial + potential_pass(near[:3], other)
        mm_some = jnp.concatenate([mm_some, other], -1)
        step *= 2
    total = sum_butterfly(sum_butterfly(partial, "rep"), "blk", low_blocks)
    pull = lax.dynamic_slice_in_dim(total[1:4], (me % low_blocks) * rows, rows, axis=1)
    known = gather_doubling(
        jnp.concatenate([total[0:1] * coupling, near], axis=0), "blk", low_blocks, blocks
    )
    potential_all = known[0]
    qm_all = known[1:4]
    atoms = qm_all.shape[1]
    species_all = known[4].astype(jnp.int32)
    live_all = ((jnp.arange(atoms) % rows).astype(jnp.float32) < known[5]).astype(jnp.float32)
    cubes = force_geometry(qm_all, mm_pos)

    picks_all = (species_all[:, None] == jnp.arange(kinds)[None, :]).astype(jnp.bfloat16)
    base_all = jnp.dot(picks_all, species_table, preferred_element_type=jnp.float32)
    start_all = (
        live_all[:, None] * (base_all + potential_all[:, None] * potential_gain[None, :])
    ).astype(jnp.bfloat16)
    live = lax.dynamic_slice_in_dim(live_all, me * rows, rows)
    potential = lax.dynamic_slice_in_dim(potential_all, me * rows, rows)
    start = lax.dynamic_slice_in_dim(start_all, me * rows, rows, axis=0)

    ghost = ghost_owner * rows + ghost_slot
    columns = jnp.arange(atoms)[None, :]
    links = jnp.zeros((rows, atoms), jnp.bfloat16)
    for k in range(ghost.shape[1]):
        links = links + (ghost[:, k : k + 1] == columns).astype(jnp.bfloat16)
    neighbour = jnp.dot(links, start_all, preferred_element_type=jnp.float32).astype(jnp.bfloat16)

    mixed = start.astype(jnp.float32) + jnp.dot(
        neighbour, message_weight, preferred_element_type=jnp.float32
    )
    before = jnp.dot(mixed.astype(jnp.bfloat16), hidden_weight, preferred_element_type=jnp.float32)
    sigma = jax.nn.sigmoid(before)
    active = before * sigma
    energy_part = live * jnp.sum(active * energy_readout[None, :], axis=1)
    charge_part = live * jnp.sum(active * charge_readout[None, :], axis=1)
    atom_energy = energy_part + charge_part * potential
    back_active = live[:, None] * (
        energy_readout[None, :] + potential[:, None] * charge_readout[None, :]
    )
    back_before = (back_active * sigma * (1.0 + before * (1.0 - sigma))).astype(jnp.bfloat16)
    back_mixed = jnp.dot(back_before, hidden_weight.T, preferred_element_type=jnp.float32)
    back_sum = jnp.dot(
        back_mixed.astype(jnp.bfloat16), message_weight.T, preferred_element_type=jnp.float32
    ).astype(jnp.bfloat16)

    sent = jnp.sum(back_sum.astype(jnp.float32) * potential_gain[None, :], axis=1)
    spread = jnp.sum(links.astype(jnp.float32) * sent[:, None], axis=0) * live_all
    local = charge_part + live * jnp.sum(back_mixed * potential_gain[None, :], axis=1)
    placed = (jnp.arange(atoms) // rows == me).astype(jnp.float32)
    local_all = jnp.tile(local, atoms // rows) * placed
    effective_all = sum_butterfly(spread + local_all, "blk")
    effective = lax.dynamic_slice_in_dim(effective_all, me * rows, rows)

    qm_force = pull * (effective * coupling)[None, :]
    mm_force = force_pass(qm_all, effective_all, mm_pos, cubes) * (-coupling * mm_charge)[None, :]
    return (atom_energy, qm_force, mm_force)


def solution(mesh):
    placed = (
        P(None, "blk"),
        P("blk"),
        P("blk"),
        P("blk", None),
        P("blk", None),
        P(None, ("blk", "rep")),
        P(("blk", "rep")),
        P(),
        P(),
        P(),
        P(),
        P(),
        P(),
    )
    return jax.shard_map(
        on_device,
        mesh=mesh,
        in_specs=placed,
        out_specs=(P("blk"), P(None, "blk"), P(None, ("blk", "rep"))),
        check_vma=False,
    )
```

```python
import jax
import jax.numpy as jnp
from jax import lax
from jax.sharding import PartitionSpec as P

SOFTEN = 0.25
CHUNK = 512


def gather_doubling(x, axis, first=1, last=None):
    n = lax.axis_size(axis)
    last = n if last is None else last
    me = lax.axis_index(axis)
    step = first
    while step < last:
        other = lax.ppermute(x, axis, [(i, i ^ step) for i in range(n)])
        low = (me // step) % 2 == 0
        x = jnp.where(low, jnp.concatenate([x, other], -1), jnp.concatenate([other, x], -1))
        step *= 2
    return x


def sum_butterfly(x, axis, last=None):
    n = lax.axis_size(axis)
    last = n if last is None else last
    step = 1
    while step < last:
        x = x + lax.ppermute(x, axis, [(i, i ^ step) for i in range(n)])
        step *= 2
    return x


def potential_pass(qm_some, mm_some):
    chunks = mm_some.shape[1] // CHUNK
    cols = [qm_some[c][None, :] for c in range(3)]

    def body(running, block):
        d = [cols[c] - block[:, c : c + 1] for c in range(3)]
        inverse = lax.rsqrt(d[0] * d[0] + d[1] * d[1] + d[2] * d[2] + SOFTEN)
        weighted = inverse * block[:, 3:4]
        cubed = weighted * inverse * inverse
        part = jnp.stack(
            [jnp.sum(weighted, axis=0)] + [jnp.sum(d[c] * cubed, axis=0) for c in range(3)]
        )
        return running + part, None

    stacked = jnp.transpose(mm_some.reshape(4, chunks, CHUNK), (1, 2, 0))
    total, _ = lax.scan(body, jnp.zeros((4, qm_some.shape[1]), jnp.float32), stacked)
    return total


def force_pass(qm_all, effective, mm_pos, scale):
    chunks = qm_all.shape[1] // CHUNK
    stacked = jnp.concatenate([qm_all, effective[None, :]], axis=0)
    stacked = jnp.transpose(stacked.reshape(4, chunks, CHUNK), (1, 2, 0))

    def body(running, block):
        d = [block[:, c : c + 1] - mm_pos[c][None, :] for c in range(3)]
        inverse = lax.rsqrt(d[0] * d[0] + d[1] * d[1] + d[2] * d[2] + SOFTEN)
        weight = inverse * inverse * inverse * block[:, 3:4] * scale[None, :]
        return running + jnp.stack([jnp.sum(d[c] * weight, axis=0) for c in range(3)]), None

    total, _ = lax.scan(body, jnp.zeros((3, mm_pos.shape[1]), jnp.float32), stacked)
    return total


def on_device(
    qm_pos,
    species,
    qm_count,
    ghost_owner,
    ghost_slot,
    mm_pos,
    mm_charge,
    species_table,
    potential_gain,
    message_weight,
    hidden_weight,
    energy_readout,
    charge_readout,
):
    rows = qm_pos.shape[1]
    blocks = lax.axis_size("blk")
    me = lax.axis_index("blk")
    kinds = species_table.shape[0]
    coupling = float(mm_pos.shape[1] * blocks * lax.axis_size("rep")) ** (-0.5)

    low_blocks = 1
    while low_blocks * low_blocks < blocks:
        low_blocks *= 2
    own = jnp.concatenate(
        [
            qm_pos,
            species.astype(jnp.float32)[None, :],
            jnp.broadcast_to(qm_count.astype(jnp.float32)[None, :], (1, rows)),
        ],
        axis=0,
    )
    near = gather_doubling(own, "blk", 1, low_blocks)
    mm_some = gather_doubling(
        jnp.concatenate([mm_pos, mm_charge[None, :]], axis=0), "blk", low_blocks, blocks
    )
    partial = potential_pass(near[:3], mm_some)
    total = sum_butterfly(sum_butterfly(partial, "rep"), "blk", low_blocks)
    pull = lax.dynamic_slice_in_dim(total[1:4], (me % low_blocks) * rows, rows, axis=1)
    known = gather_doubling(
        jnp.concatenate([total[0:1] * coupling, near], axis=0), "blk", low_blocks, blocks
    )
    potential_all = known[0]
    qm_all = known[1:4]
    atoms = qm_all.shape[1]
    species_all = known[4].astype(jnp.int32)
    live_all = ((jnp.arange(atoms) % rows).astype(jnp.float32) < known[5]).astype(jnp.float32)

    live = lax.dynamic_slice_in_dim(live_all, me * rows, rows)
    potential = lax.dynamic_slice_in_dim(potential_all, me * rows, rows)
    table_t = species_table.T
    base_t = jnp.broadcast_to(table_t[:, 0:1], (table_t.shape[0], atoms))
    for kind in range(1, kinds):
        base_t = jnp.where(species_all[None, :] == kind, table_t[:, kind : kind + 1], base_t)
    base_t = base_t.astype(jnp.float32)
    start_t = (
        live_all[None, :] * (base_t + potential_gain[:, None] * potential_all[None, :])
    ).astype(jnp.bfloat16)
    start = lax.dynamic_slice_in_dim(start_t, me * rows, rows, axis=1).T

    ghost = ghost_owner * rows + ghost_slot
    columns = jnp.arange(atoms)[None, :]
    links = jnp.zeros((rows, atoms), jnp.bfloat16)
    for k in range(ghost.shape[1]):
        links = links + (ghost[:, k : k + 1] == columns).astype(jnp.bfloat16)
    neighbour = lax.dot_general(
        links, start_t, (((1,), (1,)), ((), ())), preferred_element_type=jnp.float32
    ).astype(jnp.bfloat16)

    mixed = start.astype(jnp.float32) + jnp.dot(
        neighbour, message_weight, preferred_element_type=jnp.float32
    )
    before = jnp.dot(mixed.astype(jnp.bfloat16), hidden_weight, preferred_element_type=jnp.float32)
    sigma = jax.nn.sigmoid(before)
    active = before * sigma
    energy_part = live * jnp.sum(active * energy_readout[None, :], axis=1)
    charge_part = live * jnp.sum(active * charge_readout[None, :], axis=1)
    atom_energy = energy_part + charge_part * potential
    back_active = live[:, None] * (
        energy_readout[None, :] + potential[:, None] * charge_readout[None, :]
    )
    back_before = (back_active * sigma * (1.0 + before * (1.0 - sigma))).astype(jnp.bfloat16)
    back_mixed = jnp.dot(back_before, hidden_weight.T, preferred_element_type=jnp.float32)
    back_sum = jnp.dot(
        back_mixed.astype(jnp.bfloat16), message_weight.T, preferred_element_type=jnp.float32
    ).astype(jnp.bfloat16)

    sent = jnp.sum(back_sum.astype(jnp.float32) * potential_gain[None, :], axis=1)
    spread = jnp.sum(links.astype(jnp.float32) * sent[:, None], axis=0) * live_all
    local = charge_part + live * jnp.sum(back_mixed * potential_gain[None, :], axis=1)
    placed = (jnp.arange(atoms) // rows == me).astype(jnp.float32)
    local_all = jnp.tile(local, atoms // rows) * placed
    effective_all = sum_butterfly(spread + local_all, "blk")
    effective = lax.dynamic_slice_in_dim(effective_all, me * rows, rows)

    qm_force = pull * (effective * coupling)[None, :]
    mm_force = force_pass(qm_all, effective_all, mm_pos, -coupling * mm_charge)
    return (atom_energy, qm_force, mm_force)


def solution(mesh):
    placed = (
        P(None, "blk"),
        P("blk"),
        P("blk"),
        P("blk", None),
        P("blk", None),
        P(None, ("blk", "rep")),
        P(("blk", "rep")),
        P(),
        P(),
        P(),
        P(),
        P(),
        P(),
    )
    return jax.shard_map(
        on_device,
        mesh=mesh,
        in_specs=placed,
        out_specs=(P("blk"), P(None, "blk"), P(None, ("blk", "rep"))),
        check_vma=False,
    )
```

```python
import jax
import jax.numpy as jnp
from jax import lax
from jax.sharding import PartitionSpec as P

SOFTEN = 0.25
CHUNK = 512


def gather_doubling(x, axis, first=1, last=None):
    n = lax.axis_size(axis)
    last = n if last is None else last
    me = lax.axis_index(axis)
    step = first
    while step < last:
        other = lax.ppermute(x, axis, [(i, i ^ step) for i in range(n)])
        low = (me // step) % 2 == 0
        x = jnp.where(low, jnp.concatenate([x, other], -1), jnp.concatenate([other, x], -1))
        step *= 2
    return x


def sum_butterfly(x, axis, last=None):
    n = lax.axis_size(axis)
    last = n if last is None else last
    step = 1
    while step < last:
        x = x + lax.ppermute(x, axis, [(i, i ^ step) for i in range(n)])
        step *= 2
    return x


def potential_pass(qm_some, mm_some):
    chunks = mm_some.shape[1] // CHUNK
    cols = [qm_some[c][None, :] for c in range(3)]

    def body(running, block):
        d = [cols[c] - block[:, c : c + 1] for c in range(3)]
        inverse = lax.rsqrt(d[0] * d[0] + d[1] * d[1] + d[2] * d[2] + SOFTEN)
        weighted = inverse * block[:, 3:4]
        cubed = weighted * inverse * inverse
        part = jnp.stack(
            [jnp.sum(weighted, axis=0)] + [jnp.sum(d[c] * cubed, axis=0) for c in range(3)]
        )
        return running + part, None

    stacked = jnp.transpose(mm_some.reshape(4, chunks, CHUNK), (1, 2, 0))
    total, _ = lax.scan(body, jnp.zeros((4, qm_some.shape[1]), jnp.float32), stacked)
    return total


def force_pass(qm_all, effective, mm_pos, scale):
    chunks = qm_all.shape[1] // CHUNK
    stacked = jnp.concatenate([qm_all, effective[None, :]], axis=0)
    stacked = jnp.transpose(stacked.reshape(4, chunks, CHUNK), (1, 2, 0))

    def body(running, block):
        d = [block[:, c : c + 1] - mm_pos[c][None, :] for c in range(3)]
        inverse = lax.rsqrt(d[0] * d[0] + d[1] * d[1] + d[2] * d[2] + SOFTEN)
        weight = inverse * inverse * inverse * block[:, 3:4] * scale[None, :]
        return running + jnp.stack([jnp.sum(d[c] * weight, axis=0) for c in range(3)]), None

    total, _ = lax.scan(body, jnp.zeros((3, mm_pos.shape[1]), jnp.float32), stacked)
    return total


def on_device(
    qm_pos,
    species,
    qm_count,
    ghost_owner,
    ghost_slot,
    mm_pos,
    mm_charge,
    species_table,
    potential_gain,
    message_weight,
    hidden_weight,
    energy_readout,
    charge_readout,
):
    rows = qm_pos.shape[1]
    blocks = lax.axis_size("blk")
    me = lax.axis_index("blk")
    kinds = species_table.shape[0]
    coupling = float(mm_pos.shape[1] * blocks * lax.axis_size("rep")) ** (-0.5)

    low_blocks = 1
    while low_blocks * low_blocks < blocks:
        low_blocks *= 2
    own = jnp.concatenate(
        [
            qm_pos,
            species.astype(jnp.float32)[None, :],
            jnp.broadcast_to(qm_count.astype(jnp.float32)[None, :], (1, rows)),
        ],
        axis=0,
    )
    near = gather_doubling(own, "blk", 1, low_blocks)
    mm_some = gather_doubling(
        jnp.concatenate([mm_pos, mm_charge[None, :]], axis=0), "blk", low_blocks, blocks
    )
    partial = potential_pass(near[:3], mm_some)
    total = sum_butterfly(sum_butterfly(partial, "rep"), "blk", low_blocks)
    pull = lax.dynamic_slice_in_dim(total[1:4], (me % low_blocks) * rows, rows, axis=1)
    known = gather_doubling(
        jnp.concatenate([total[0:1] * coupling, near], axis=0), "blk", low_blocks, blocks
    )
    potential_all = known[0]
    qm_all = known[1:4]
    atoms = qm_all.shape[1]
    species_all = known[4].astype(jnp.int32)
    live_all = ((jnp.arange(atoms) % rows).astype(jnp.float32) < known[5]).astype(jnp.float32)

    live = lax.dynamic_slice_in_dim(live_all, me * rows, rows)
    potential = lax.dynamic_slice_in_dim(potential_all, me * rows, rows)
    picks_t = (jnp.arange(kinds)[:, None] == species_all[None, :]).astype(jnp.bfloat16)
    base_t = jnp.dot(species_table.T, picks_t, preferred_element_type=jnp.float32)
    start_t = (
        live_all[None, :] * (base_t + potential_gain[:, None] * potential_all[None, :])
    ).astype(jnp.bfloat16)
    start = lax.dynamic_slice_in_dim(start_t, me * rows, rows, axis=1).T

    ghost = ghost_owner * rows + ghost_slot
    columns = jnp.arange(atoms)[None, :]
    links = jnp.zeros((rows, atoms), jnp.bfloat16)
    for k in range(ghost.shape[1]):
        links = links + (ghost[:, k : k + 1] == columns).astype(jnp.bfloat16)
    neighbour = lax.dot_general(
        links, start_t, (((1,), (1,)), ((), ())), preferred_element_type=jnp.float32
    ).astype(jnp.bfloat16)

    mixed = start.astype(jnp.float32) + jnp.dot(
        neighbour, message_weight, preferred_element_type=jnp.float32
    )
    before = jnp.dot(mixed.astype(jnp.bfloat16), hidden_weight, preferred_element_type=jnp.float32)
    sigma = jax.nn.sigmoid(before)
    active = before * sigma
    energy_part = live * jnp.sum(active * energy_readout[None, :], axis=1)
    charge_part = live * jnp.sum(active * charge_readout[None, :], axis=1)
    atom_energy = energy_part + charge_part * potential
    back_active = live[:, None] * (
        energy_readout[None, :] + potential[:, None] * charge_readout[None, :]
    )
    back_before = (back_active * sigma * (1.0 + before * (1.0 - sigma))).astype(jnp.bfloat16)
    back_mixed = jnp.dot(back_before, hidden_weight.T, preferred_element_type=jnp.float32)
    back_sum = jnp.dot(
        back_mixed.astype(jnp.bfloat16), message_weight.T, preferred_element_type=jnp.float32
    ).astype(jnp.bfloat16)

    sent = jnp.sum(back_sum.astype(jnp.float32) * potential_gain[None, :], axis=1)
    spread = jnp.sum(links.astype(jnp.float32) * sent[:, None], axis=0) * live_all
    local = charge_part + live * jnp.sum(back_mixed * potential_gain[None, :], axis=1)
    placed = (jnp.arange(atoms) // rows == me).astype(jnp.float32)
    local_all = jnp.tile(local, atoms // rows) * placed
    effective_all = sum_butterfly(spread + local_all, "blk")
    effective = lax.dynamic_slice_in_dim(effective_all, me * rows, rows)

    qm_force = pull * (effective * coupling)[None, :]
    mm_force = force_pass(qm_all, effective_all, mm_pos, -coupling * mm_charge)
    return (atom_energy, qm_force, mm_force)


def solution(mesh):
    placed = (
        P(None, "blk"),
        P("blk"),
        P("blk"),
        P("blk", None),
        P("blk", None),
        P(None, ("blk", "rep")),
        P(("blk", "rep")),
        P(),
        P(),
        P(),
        P(),
        P(),
        P(),
    )
    return jax.shard_map(
        on_device,
        mesh=mesh,
        in_specs=placed,
        out_specs=(P("blk"), P(None, "blk"), P(None, ("blk", "rep"))),
        check_vma=False,
    )
```

```python
import jax
import jax.numpy as jnp
from jax import lax
from jax.sharding import PartitionSpec as P

SOFTEN = 0.25
CHUNK = 512


def gather_doubling(x, axis, first=1, last=None):
    n = lax.axis_size(axis)
    last = n if last is None else last
    me = lax.axis_index(axis)
    step = first
    while step < last:
        other = lax.ppermute(x, axis, [(i, i ^ step) for i in range(n)])
        low = (me // step) % 2 == 0
        x = jnp.where(low, jnp.concatenate([x, other], -1), jnp.concatenate([other, x], -1))
        step *= 2
    return x


def sum_butterfly(x, axis, last=None):
    n = lax.axis_size(axis)
    last = n if last is None else last
    step = 1
    while step < last:
        x = x + lax.ppermute(x, axis, [(i, i ^ step) for i in range(n)])
        step *= 2
    return x


def potential_pass(qm_some, mm_some):
    chunks = mm_some.shape[1] // CHUNK
    cols = [qm_some[c][None, :] for c in range(3)]

    def body(running, block):
        d = [cols[c] - block[:, c : c + 1] for c in range(3)]
        inverse = lax.rsqrt(d[0] * d[0] + d[1] * d[1] + d[2] * d[2] + SOFTEN)
        weighted = inverse * block[:, 3:4]
        cubed = weighted * inverse * inverse
        part = jnp.stack(
            [jnp.sum(weighted, axis=0)] + [jnp.sum(d[c] * cubed, axis=0) for c in range(3)]
        )
        return running + part, None

    stacked = jnp.transpose(mm_some.reshape(4, chunks, CHUNK), (1, 2, 0))
    total, _ = lax.scan(body, jnp.zeros((4, qm_some.shape[1]), jnp.float32), stacked)
    return total


def force_pass(qm_all, effective, mm_pos, scale):
    chunks = qm_all.shape[1] // CHUNK
    stacked = jnp.concatenate([qm_all, effective[None, :]], axis=0)
    stacked = jnp.transpose(stacked.reshape(4, chunks, CHUNK), (1, 2, 0))

    def body(running, block):
        d = [block[:, c : c + 1] - mm_pos[c][None, :] for c in range(3)]
        inverse = lax.rsqrt(d[0] * d[0] + d[1] * d[1] + d[2] * d[2] + SOFTEN)
        weight = inverse * inverse * inverse * block[:, 3:4] * scale[None, :]
        return running + jnp.stack([jnp.sum(d[c] * weight, axis=0) for c in range(3)]), None

    total, _ = lax.scan(body, jnp.zeros((3, mm_pos.shape[1]), jnp.float32), stacked)
    return total


def on_device(
    qm_pos,
    species,
    qm_count,
    ghost_owner,
    ghost_slot,
    mm_pos,
    mm_charge,
    species_table,
    potential_gain,
    message_weight,
    hidden_weight,
    energy_readout,
    charge_readout,
):
    rows = qm_pos.shape[1]
    blocks = lax.axis_size("blk")
    me = lax.axis_index("blk")
    kinds = species_table.shape[0]
    coupling = float(mm_pos.shape[1] * blocks * lax.axis_size("rep")) ** (-0.5)

    low_blocks = 1
    while low_blocks * low_blocks < blocks:
        low_blocks *= 2
    own = jnp.concatenate(
        [
            qm_pos,
            species.astype(jnp.float32)[None, :],
            jnp.broadcast_to(qm_count.astype(jnp.float32)[None, :], (1, rows)),
        ],
        axis=0,
    )
    near = gather_doubling(own, "blk", 1, low_blocks)
    near, table_t = lax.optimization_barrier((near, species_table.T))
    mm_some = gather_doubling(
        jnp.concatenate([mm_pos, mm_charge[None, :]], axis=0), "blk", low_blocks, blocks
    )
    partial = potential_pass(near[:3], mm_some)
    total = sum_butterfly(sum_butterfly(partial, "rep"), "blk", low_blocks)
    pull = lax.dynamic_slice_in_dim(total[1:4], (me % low_blocks) * rows, rows, axis=1)
    known = gather_doubling(
        jnp.concatenate([total[0:1] * coupling, near], axis=0), "blk", low_blocks, blocks
    )
    potential_all = known[0]
    qm_all = known[1:4]
    atoms = qm_all.shape[1]
    species_all = known[4].astype(jnp.int32)
    live_all = ((jnp.arange(atoms) % rows).astype(jnp.float32) < known[5]).astype(jnp.float32)

    live = lax.dynamic_slice_in_dim(live_all, me * rows, rows)
    potential = lax.dynamic_slice_in_dim(potential_all, me * rows, rows)
    picks_t = (jnp.arange(kinds)[:, None] == species_all[None, :]).astype(jnp.bfloat16)
    base_t = jnp.dot(table_t, picks_t, preferred_element_type=jnp.float32)
    start_t = (
        live_all[None, :] * (base_t + potential_gain[:, None] * potential_all[None, :])
    ).astype(jnp.bfloat16)
    start = lax.dynamic_slice_in_dim(start_t, me * rows, rows, axis=1).T

    ghost = ghost_owner * rows + ghost_slot
    columns = jnp.arange(atoms)[None, :]
    links = jnp.zeros((rows, atoms), jnp.bfloat16)
    for k in range(ghost.shape[1]):
        links = links + (ghost[:, k : k + 1] == columns).astype(jnp.bfloat16)
    neighbour = lax.dot_general(
        links, start_t, (((1,), (1,)), ((), ())), preferred_element_type=jnp.float32
    ).astype(jnp.bfloat16)

    mixed = start.astype(jnp.float32) + jnp.dot(
        neighbour, message_weight, preferred_element_type=jnp.float32
    )
    before = jnp.dot(mixed.astype(jnp.bfloat16), hidden_weight, preferred_element_type=jnp.float32)
    sigma = jax.nn.sigmoid(before)
    active = before * sigma
    energy_part = live * jnp.sum(active * energy_readout[None, :], axis=1)
    charge_part = live * jnp.sum(active * charge_readout[None, :], axis=1)
    atom_energy = energy_part + charge_part * potential
    back_active = live[:, None] * (
        energy_readout[None, :] + potential[:, None] * charge_readout[None, :]
    )
    back_before = (back_active * sigma * (1.0 + before * (1.0 - sigma))).astype(jnp.bfloat16)
    back_mixed = jnp.dot(back_before, hidden_weight.T, preferred_element_type=jnp.float32)
    back_sum = jnp.dot(
        back_mixed.astype(jnp.bfloat16), message_weight.T, preferred_element_type=jnp.float32
    ).astype(jnp.bfloat16)

    sent = jnp.sum(back_sum.astype(jnp.float32) * potential_gain[None, :], axis=1)
    spread = jnp.sum(links.astype(jnp.float32) * sent[:, None], axis=0) * live_all
    local = charge_part + live * jnp.sum(back_mixed * potential_gain[None, :], axis=1)
    placed = (jnp.arange(atoms) // rows == me).astype(jnp.float32)
    local_all = jnp.tile(local, atoms // rows) * placed
    part = sum_butterfly(spread + local_all, "blk", blocks // 2)
    other = lax.ppermute(part, "blk", [(i, i ^ (blocks // 2)) for i in range(blocks)])
    effective_all = part + other
    effective = lax.dynamic_slice_in_dim(part, me * rows, rows) + lax.dynamic_slice_in_dim(
        other, me * rows, rows
    )
    qm_force = pull * (effective * coupling)[None, :]
    mm_force = force_pass(qm_all, effective_all, mm_pos, -coupling * mm_charge)
    return (atom_energy, qm_force, mm_force)


def solution(mesh):
    placed = (
        P(None, "blk"),
        P("blk"),
        P("blk"),
        P("blk", None),
        P("blk", None),
        P(None, ("blk", "rep")),
        P(("blk", "rep")),
        P(),
        P(),
        P(),
        P(),
        P(),
        P(),
    )
    return jax.shard_map(
        on_device,
        mesh=mesh,
        in_specs=placed,
        out_specs=(P("blk"), P(None, "blk"), P(None, ("blk", "rep"))),
        check_vma=False,
    )
```

```python
import jax
import jax.numpy as jnp
from jax import lax
from jax.sharding import PartitionSpec as P

SOFTEN = 0.25
CHUNK = 512
WHOLE = True


def gather_doubling(x, axis, first=1, last=None):
    n = lax.axis_size(axis)
    last = n if last is None else last
    me = lax.axis_index(axis)
    step = first
    while step < last:
        other = lax.ppermute(x, axis, [(i, i ^ step) for i in range(n)])
        low = (me // step) % 2 == 0
        x = jnp.where(low, jnp.concatenate([x, other], -1), jnp.concatenate([other, x], -1))
        step *= 2
    return x


def sum_butterfly(x, axis, last=None):
    n = lax.axis_size(axis)
    last = n if last is None else last
    step = 1
    while step < last:
        x = x + lax.ppermute(x, axis, [(i, i ^ step) for i in range(n)])
        step *= 2
    return x


def potential_pass(qm_some, mm_some):
    chunks = 1 if WHOLE else mm_some.shape[1] // CHUNK
    cols = [qm_some[c][None, :] for c in range(3)]

    def body(running, block):
        d = [cols[c] - block[:, c : c + 1] for c in range(3)]
        inverse = lax.rsqrt(d[0] * d[0] + d[1] * d[1] + d[2] * d[2] + SOFTEN)
        weighted = inverse * block[:, 3:4]
        cubed = weighted * inverse * inverse
        part = jnp.stack(
            [jnp.sum(weighted, axis=0)] + [jnp.sum(d[c] * cubed, axis=0) for c in range(3)]
        )
        return running + part, None

    stacked = jnp.transpose(mm_some.reshape(4, chunks, -1), (1, 2, 0))
    total, _ = lax.scan(body, jnp.zeros((4, qm_some.shape[1]), jnp.float32), stacked)
    return total


def force_pass(qm_all, effective, mm_pos, scale):
    chunks = 1 if WHOLE else qm_all.shape[1] // CHUNK
    stacked = jnp.concatenate([qm_all, effective[None, :]], axis=0)
    stacked = jnp.transpose(stacked.reshape(4, chunks, -1), (1, 2, 0))

    def body(running, block):
        d = [block[:, c : c + 1] - mm_pos[c][None, :] for c in range(3)]
        inverse = lax.rsqrt(d[0] * d[0] + d[1] * d[1] + d[2] * d[2] + SOFTEN)
        weight = inverse * inverse * inverse * block[:, 3:4] * scale[None, :]
        return running + jnp.stack([jnp.sum(d[c] * weight, axis=0) for c in range(3)]), None

    total, _ = lax.scan(body, jnp.zeros((3, mm_pos.shape[1]), jnp.float32), stacked)
    return total


def on_device(
    qm_pos,
    species,
    qm_count,
    ghost_owner,
    ghost_slot,
    mm_pos,
    mm_charge,
    species_table,
    potential_gain,
    message_weight,
    hidden_weight,
    energy_readout,
    charge_readout,
):
    rows = qm_pos.shape[1]
    blocks = lax.axis_size("blk")
    me = lax.axis_index("blk")
    kinds = species_table.shape[0]
    coupling = float(mm_pos.shape[1] * blocks * lax.axis_size("rep")) ** (-0.5)

    low_blocks = 1
    while low_blocks * low_blocks < blocks:
        low_blocks *= 2
    own = jnp.concatenate(
        [
            qm_pos,
            species.astype(jnp.float32)[None, :],
            jnp.broadcast_to(qm_count.astype(jnp.float32)[None, :], (1, rows)),
        ],
        axis=0,
    )
    near = gather_doubling(own, "blk", 1, low_blocks)
    near, table_t = lax.optimization_barrier((near, species_table.T))
    mm_some = gather_doubling(
        jnp.concatenate([mm_pos, mm_charge[None, :]], axis=0), "blk", low_blocks, blocks
    )
    partial = potential_pass(near[:3], mm_some)
    total = sum_butterfly(sum_butterfly(partial, "rep"), "blk", low_blocks)
    pull = lax.dynamic_slice_in_dim(total[1:4], (me % low_blocks) * rows, rows, axis=1)
    known = gather_doubling(
        jnp.concatenate([total[0:1] * coupling, near], axis=0), "blk", low_blocks, blocks
    )
    potential_all = known[0]
    qm_all = known[1:4]
    atoms = qm_all.shape[1]
    species_all = known[4].astype(jnp.int32)
    live_all = ((jnp.arange(atoms) % rows).astype(jnp.float32) < known[5]).astype(jnp.float32)

    live = lax.dynamic_slice_in_dim(live_all, me * rows, rows)
    potential = lax.dynamic_slice_in_dim(potential_all, me * rows, rows)
    picks_t = (jnp.arange(kinds)[:, None] == species_all[None, :]).astype(jnp.bfloat16)
    base_t = jnp.dot(table_t, picks_t, preferred_element_type=jnp.float32)
    start_t = (
        live_all[None, :] * (base_t + potential_gain[:, None] * potential_all[None, :])
    ).astype(jnp.bfloat16)
    start = lax.dynamic_slice_in_dim(start_t, me * rows, rows, axis=1).T

    ghost = ghost_owner * rows + ghost_slot
    columns = jnp.arange(atoms)[None, :]
    links = jnp.zeros((rows, atoms), jnp.bfloat16)
    for k in range(ghost.shape[1]):
        links = links + (ghost[:, k : k + 1] == columns).astype(jnp.bfloat16)
    neighbour = lax.dot_general(
        links, start_t, (((1,), (1,)), ((), ())), preferred_element_type=jnp.float32
    ).astype(jnp.bfloat16)

    mixed = start.astype(jnp.float32) + jnp.dot(
        neighbour, message_weight, preferred_element_type=jnp.float32
    )
    before = jnp.dot(mixed.astype(jnp.bfloat16), hidden_weight, preferred_element_type=jnp.float32)
    sigma = jax.nn.sigmoid(before)
    active = before * sigma
    energy_part = live * jnp.sum(active * energy_readout[None, :], axis=1)
    charge_part = live * jnp.sum(active * charge_readout[None, :], axis=1)
    atom_energy = energy_part + charge_part * potential
    back_active = live[:, None] * (
        energy_readout[None, :] + potential[:, None] * charge_readout[None, :]
    )
    back_before = (back_active * sigma * (1.0 + before * (1.0 - sigma))).astype(jnp.bfloat16)
    back_mixed = jnp.dot(back_before, hidden_weight.T, preferred_element_type=jnp.float32)
    back_sum = jnp.dot(
        back_mixed.astype(jnp.bfloat16), message_weight.T, preferred_element_type=jnp.float32
    ).astype(jnp.bfloat16)

    sent = jnp.sum(back_sum.astype(jnp.float32) * potential_gain[None, :], axis=1)
    spread = jnp.sum(links.astype(jnp.float32) * sent[:, None], axis=0) * live_all
    local = charge_part + live * jnp.sum(back_mixed * potential_gain[None, :], axis=1)
    placed = (jnp.arange(atoms) // rows == me).astype(jnp.float32)
    local_all = jnp.tile(local, atoms // rows) * placed
    part = sum_butterfly(spread + local_all, "blk", blocks // 2)
    other = lax.ppermute(part, "blk", [(i, i ^ (blocks // 2)) for i in range(blocks)])
    effective_all = part + other
    effective = lax.dynamic_slice_in_dim(part, me * rows, rows) + lax.dynamic_slice_in_dim(
        other, me * rows, rows
    )
    qm_force = pull * (effective * coupling)[None, :]
    mm_force = force_pass(qm_all, effective_all, mm_pos, -coupling * mm_charge)
    return (atom_energy, qm_force, mm_force)


def solution(mesh):
    placed = (
        P(None, "blk"),
        P("blk"),
        P("blk"),
        P("blk", None),
        P("blk", None),
        P(None, ("blk", "rep")),
        P(("blk", "rep")),
        P(),
        P(),
        P(),
        P(),
        P(),
        P(),
    )
    return jax.shard_map(
        on_device,
        mesh=mesh,
        in_specs=placed,
        out_specs=(P("blk"), P(None, "blk"), P(None, ("blk", "rep"))),
        check_vma=False,
    )
```

```python
import jax
import jax.numpy as jnp
from jax import lax
from jax.experimental import pallas as pl
from jax.experimental.pallas import tpu as pltpu
from jax.sharding import PartitionSpec as P

SOFTEN = 0.25
CHUNK = 512


def gather_doubling(x, axis, first=1, last=None):
    n = lax.axis_size(axis)
    last = n if last is None else last
    me = lax.axis_index(axis)
    step = first
    while step < last:
        other = lax.ppermute(x, axis, [(i, i ^ step) for i in range(n)])
        low = (me // step) % 2 == 0
        x = jnp.where(low, jnp.concatenate([x, other], -1), jnp.concatenate([other, x], -1))
        step *= 2
    return x


def sum_butterfly(x, axis, last=None):
    n = lax.axis_size(axis)
    last = n if last is None else last
    step = 1
    while step < last:
        x = x + lax.ppermute(x, axis, [(i, i ^ step) for i in range(n)])
        step *= 2
    return x


def potential_pass(qm_some, mm_some):
    chunks = mm_some.shape[1] // CHUNK
    cols = [qm_some[c][None, :] for c in range(3)]

    def body(running, block):
        d = [cols[c] - block[:, c : c + 1] for c in range(3)]
        inverse = lax.rsqrt(d[0] * d[0] + d[1] * d[1] + d[2] * d[2] + SOFTEN)
        weighted = inverse * block[:, 3:4]
        cubed = weighted * inverse * inverse
        part = jnp.stack(
            [jnp.sum(weighted, axis=0)] + [jnp.sum(d[c] * cubed, axis=0) for c in range(3)]
        )
        return running + part, None

    stacked = jnp.transpose(mm_some.reshape(4, chunks, CHUNK), (1, 2, 0))
    total, _ = lax.scan(body, jnp.zeros((4, qm_some.shape[1]), jnp.float32), stacked)
    return total


def force_pass(qm_all, effective, mm_pos, scale):
    chunks = qm_all.shape[1] // CHUNK
    stacked = jnp.concatenate([qm_all, effective[None, :]], axis=0)
    stacked = jnp.transpose(stacked.reshape(4, chunks, CHUNK), (1, 2, 0))

    def body(running, block):
        d = [block[:, c : c + 1] - mm_pos[c][None, :] for c in range(3)]
        inverse = lax.rsqrt(d[0] * d[0] + d[1] * d[1] + d[2] * d[2] + SOFTEN)
        weight = inverse * inverse * inverse * block[:, 3:4] * scale[None, :]
        return running + jnp.stack([jnp.sum(d[c] * weight, axis=0) for c in range(3)]), None

    total, _ = lax.scan(body, jnp.zeros((3, mm_pos.shape[1]), jnp.float32), stacked)
    return total


def network_kernel(
    ghost_ref, start_t_ref, start_ref, live_ref, pot_ref, live_all_ref,
    mw_ref, hw_ref, er_ref, cr_ref, pg_ref, energy_ref, spread_ref, local_ref,
):
    rows, atoms = ghost_ref.shape[0], start_t_ref.shape[1]
    columns = lax.broadcasted_iota(jnp.int32, (rows, atoms), 1)
    links = jnp.zeros((rows, atoms), jnp.float32)
    for k in range(ghost_ref.shape[1]):
        links = links + (ghost_ref[:, k : k + 1] == columns).astype(jnp.float32)
    contract_last = (((1,), (1,)), ((), ()))
    neighbour = lax.dot_general(
        links.astype(jnp.bfloat16), start_t_ref[...], contract_last,
        preferred_element_type=jnp.float32,
    ).astype(jnp.bfloat16)
    mw = mw_ref[...]
    hw = hw_ref[...]
    er = er_ref[...]
    cr = cr_ref[...]
    pg = pg_ref[...]
    live = live_ref[...]
    potential = pot_ref[...]
    mixed = start_ref[...].astype(jnp.float32) + jnp.dot(
        neighbour, mw, preferred_element_type=jnp.float32
    )
    before = jnp.dot(mixed.astype(jnp.bfloat16), hw, preferred_element_type=jnp.float32)
    sigma = jax.nn.sigmoid(before)
    active = before * sigma
    energy_part = live * jnp.sum(active * er, axis=1, keepdims=True)
    charge_part = live * jnp.sum(active * cr, axis=1, keepdims=True)
    energy_ref[...] = energy_part + charge_part * potential
    back_active = live * (er + potential * cr)
    back_before = (back_active * sigma * (1.0 + before * (1.0 - sigma))).astype(jnp.bfloat16)
    back_mixed = lax.dot_general(back_before, hw, contract_last, preferred_element_type=jnp.float32)
    back_sum = lax.dot_general(
        back_mixed.astype(jnp.bfloat16), mw, contract_last, preferred_element_type=jnp.float32
    ).astype(jnp.bfloat16)
    sent = jnp.sum(back_sum.astype(jnp.float32) * pg, axis=1, keepdims=True)
    spread_ref[...] = jnp.sum(links * sent, axis=0, keepdims=True) * live_all_ref[...]
    local_ref[...] = charge_part + live * jnp.sum(back_mixed * pg, axis=1, keepdims=True)


def network(ghost, start_t, start, live, potential, live_all, mw, hw, er, cr, pg):
    rows, atoms = ghost.shape[0], start_t.shape[1]
    vmem = pl.BlockSpec(memory_space=pltpu.VMEM)
    return pl.pallas_call(
        network_kernel,
        out_shape=(
            jax.ShapeDtypeStruct((rows, 1), jnp.float32),
            jax.ShapeDtypeStruct((1, atoms), jnp.float32),
            jax.ShapeDtypeStruct((rows, 1), jnp.float32),
        ),
        in_specs=[vmem] * 11,
        out_specs=(vmem, vmem, vmem),
        cost_estimate=pl.CostEstimate(
            flops=2 * rows * (atoms * 128 + 4 * 128 * 256), transcendentals=rows * 256,
            bytes_accessed=atoms * 128 * 2 + 4 * 128 * 256,
        ),
    )(ghost, start_t, start, live[:, None], potential[:, None], live_all[None, :],
      mw, hw, er[None, :], cr[None, :], pg[None, :])


def on_device(
    qm_pos,
    species,
    qm_count,
    ghost_owner,
    ghost_slot,
    mm_pos,
    mm_charge,
    species_table,
    potential_gain,
    message_weight,
    hidden_weight,
    energy_readout,
    charge_readout,
):
    rows = qm_pos.shape[1]
    blocks = lax.axis_size("blk")
    me = lax.axis_index("blk")
    kinds = species_table.shape[0]
    coupling = float(mm_pos.shape[1] * blocks * lax.axis_size("rep")) ** (-0.5)

    low_blocks = 1
    while low_blocks * low_blocks < blocks:
        low_blocks *= 2
    own = jnp.concatenate(
        [
            qm_pos,
            species.astype(jnp.float32)[None, :],
            jnp.broadcast_to(qm_count.astype(jnp.float32)[None, :], (1, rows)),
        ],
        axis=0,
    )
    near = gather_doubling(own, "blk", 1, low_blocks)
    near, table_t = lax.optimization_barrier((near, species_table.T))
    mm_some = gather_doubling(
        jnp.concatenate([mm_pos, mm_charge[None, :]], axis=0), "blk", low_blocks, blocks
    )
    partial = potential_pass(near[:3], mm_some)
    total = sum_butterfly(sum_butterfly(partial, "rep"), "blk", low_blocks)
    pull = lax.dynamic_slice_in_dim(total[1:4], (me % low_blocks) * rows, rows, axis=1)
    known = gather_doubling(
        jnp.concatenate([total[0:1] * coupling, near], axis=0), "blk", low_blocks, blocks
    )
    potential_all = known[0]
    qm_all = known[1:4]
    atoms = qm_all.shape[1]
    species_all = known[4].astype(jnp.int32)
    live_all = ((jnp.arange(atoms) % rows).astype(jnp.float32) < known[5]).astype(jnp.float32)

    live = lax.dynamic_slice_in_dim(live_all, me * rows, rows)
    potential = lax.dynamic_slice_in_dim(potential_all, me * rows, rows)
    picks_t = (jnp.arange(kinds)[:, None] == species_all[None, :]).astype(jnp.bfloat16)
    base_t = jnp.dot(table_t, picks_t, preferred_element_type=jnp.float32)
    start_t = (
        live_all[None, :] * (base_t + potential_gain[:, None] * potential_all[None, :])
    ).astype(jnp.bfloat16)
    start = lax.dynamic_slice_in_dim(start_t, me * rows, rows, axis=1).T

    ghost = ghost_owner * rows + ghost_slot
    energy_col, spread_row, local_col = network(
        ghost, start_t, start, live, potential, live_all, message_weight, hidden_weight,
        energy_readout, charge_readout, potential_gain,
    )
    atom_energy = energy_col[:, 0]
    spread = spread_row[0]
    local = local_col[:, 0]
    placed = (jnp.arange(atoms) // rows == me).astype(jnp.float32)
    local_all = jnp.tile(local, atoms // rows) * placed
    part = sum_butterfly(spread + local_all, "blk", blocks // 2)
    other = lax.ppermute(part, "blk", [(i, i ^ (blocks // 2)) for i in range(blocks)])
    effective_all = part + other
    effective = lax.dynamic_slice_in_dim(part, me * rows, rows) + lax.dynamic_slice_in_dim(
        other, me * rows, rows
    )
    qm_force = pull * (effective * coupling)[None, :]
    mm_force = force_pass(qm_all, effective_all, mm_pos, -coupling * mm_charge)
    return (atom_energy, qm_force, mm_force)


def solution(mesh):
    placed = (
        P(None, "blk"),
        P("blk"),
        P("blk"),
        P("blk", None),
        P("blk", None),
        P(None, ("blk", "rep")),
        P(("blk", "rep")),
        P(),
        P(),
        P(),
        P(),
        P(),
        P(),
    )
    return jax.shard_map(
        on_device,
        mesh=mesh,
        in_specs=placed,
        out_specs=(P("blk"), P(None, "blk"), P(None, ("blk", "rep"))),
        check_vma=False,
    )
```

```python
import jax
import jax.numpy as jnp
from jax import lax
from jax.sharding import PartitionSpec as P

SOFTEN = 0.25
CHUNK = 1024


def gather_doubling(x, axis, first=1, last=None):
    n = lax.axis_size(axis)
    last = n if last is None else last
    me = lax.axis_index(axis)
    step = first
    while step < last:
        other = lax.ppermute(x, axis, [(i, i ^ step) for i in range(n)])
        low = (me // step) % 2 == 0
        x = jnp.where(low, jnp.concatenate([x, other], -1), jnp.concatenate([other, x], -1))
        step *= 2
    return x


def sum_butterfly(x, axis, last=None):
    n = lax.axis_size(axis)
    last = n if last is None else last
    step = 1
    while step < last:
        x = x + lax.ppermute(x, axis, [(i, i ^ step) for i in range(n)])
        step *= 2
    return x


def potential_pass(qm_some, mm_some):
    chunks = max(1, mm_some.shape[1] // CHUNK)
    cols = [qm_some[c][None, :] for c in range(3)]

    def body(running, block):
        d = [cols[c] - block[:, c : c + 1] for c in range(3)]
        inverse = lax.rsqrt(d[0] * d[0] + d[1] * d[1] + d[2] * d[2] + SOFTEN)
        weighted = inverse * block[:, 3:4]
        cubed = weighted * inverse * inverse
        part = jnp.stack(
            [jnp.sum(weighted, axis=0)] + [jnp.sum(d[c] * cubed, axis=0) for c in range(3)]
        )
        return running + part, None

    stacked = jnp.transpose(mm_some.reshape(4, chunks, -1), (1, 2, 0))
    total, _ = lax.scan(body, jnp.zeros((4, qm_some.shape[1]), jnp.float32), stacked)
    return total


def force_pass(qm_all, effective, mm_pos, scale):
    chunks = max(1, qm_all.shape[1] // CHUNK)
    stacked = jnp.concatenate([qm_all, effective[None, :]], axis=0)
    stacked = jnp.transpose(stacked.reshape(4, chunks, -1), (1, 2, 0))

    def body(running, block):
        d = [block[:, c : c + 1] - mm_pos[c][None, :] for c in range(3)]
        inverse = lax.rsqrt(d[0] * d[0] + d[1] * d[1] + d[2] * d[2] + SOFTEN)
        weight = inverse * inverse * inverse * block[:, 3:4] * scale[None, :]
        return running + jnp.stack([jnp.sum(d[c] * weight, axis=0) for c in range(3)]), None

    total, _ = lax.scan(body, jnp.zeros((3, mm_pos.shape[1]), jnp.float32), stacked)
    return total


def on_device(
    qm_pos,
    species,
    qm_count,
    ghost_owner,
    ghost_slot,
    mm_pos,
    mm_charge,
    species_table,
    potential_gain,
    message_weight,
    hidden_weight,
    energy_readout,
    charge_readout,
):
    rows = qm_pos.shape[1]
    blocks = lax.axis_size("blk")
    me = lax.axis_index("blk")
    kinds = species_table.shape[0]
    coupling = float(mm_pos.shape[1] * blocks * lax.axis_size("rep")) ** (-0.5)

    low_blocks = 1
    while low_blocks * low_blocks < blocks:
        low_blocks *= 2
    own = jnp.concatenate(
        [
            qm_pos,
            species.astype(jnp.float32)[None, :],
            jnp.broadcast_to(qm_count.astype(jnp.float32)[None, :], (1, rows)),
        ],
        axis=0,
    )
    near = gather_doubling(own, "blk", 1, low_blocks)
    near, table_t, mixing = lax.optimization_barrier(
        (near, species_table.T.astype(jnp.float32), message_weight.astype(jnp.float32))
    )
    mm_some = gather_doubling(
        jnp.concatenate([mm_pos, mm_charge[None, :]], axis=0), "blk", low_blocks, blocks
    )
    partial = potential_pass(near[:3], mm_some)
    total = sum_butterfly(sum_butterfly(partial, "rep"), "blk", low_blocks)
    pull = lax.dynamic_slice_in_dim(total[1:4], (me % low_blocks) * rows, rows, axis=1)
    known = gather_doubling(
        jnp.concatenate([total[0:1] * coupling, near], axis=0), "blk", low_blocks, blocks
    )
    potential_all = known[0]
    qm_all = known[1:4]
    atoms = qm_all.shape[1]
    species_all = known[4].astype(jnp.int32)
    live_all = ((jnp.arange(atoms) % rows).astype(jnp.float32) < known[5]).astype(jnp.float32)

    live = lax.dynamic_slice_in_dim(live_all, me * rows, rows)
    potential = lax.dynamic_slice_in_dim(potential_all, me * rows, rows)
    picks_t = (jnp.arange(kinds)[:, None] == species_all[None, :]).astype(jnp.bfloat16)
    base_t = jnp.dot(table_t, picks_t.astype(jnp.float32), preferred_element_type=jnp.float32)
    start_t = (
        live_all[None, :] * (base_t + potential_gain[:, None] * potential_all[None, :])
    ).astype(jnp.bfloat16)
    start = lax.dynamic_slice_in_dim(start_t, me * rows, rows, axis=1).T

    ghost = ghost_owner * rows + ghost_slot
    columns = jnp.arange(atoms)[None, :]
    links = jnp.zeros((rows, atoms), jnp.bfloat16)
    for k in range(ghost.shape[1]):
        links = links + (ghost[:, k : k + 1] == columns).astype(jnp.bfloat16)
    neighbour = lax.dot_general(
        links, start_t, (((1,), (1,)), ((), ())), preferred_element_type=jnp.float32
    ).astype(jnp.bfloat16)

    mixed = start.astype(jnp.float32) + jnp.dot(
        neighbour.astype(jnp.float32), mixing, preferred_element_type=jnp.float32
    )
    before = jnp.dot(mixed.astype(jnp.bfloat16), hidden_weight, preferred_element_type=jnp.float32)
    sigma = jax.nn.sigmoid(before)
    active = before * sigma
    energy_part = live * jnp.sum(active * energy_readout[None, :], axis=1)
    charge_part = live * jnp.sum(active * charge_readout[None, :], axis=1)
    atom_energy = energy_part + charge_part * potential
    back_active = live[:, None] * (
        energy_readout[None, :] + potential[:, None] * charge_readout[None, :]
    )
    back_before = (back_active * sigma * (1.0 + before * (1.0 - sigma))).astype(jnp.bfloat16)
    back_mixed = jnp.dot(back_before, hidden_weight.T, preferred_element_type=jnp.float32)
    back_sum = jnp.dot(
        back_mixed.astype(jnp.bfloat16).astype(jnp.float32), mixing.T,
        preferred_element_type=jnp.float32,
    ).astype(jnp.bfloat16)

    sent = jnp.sum(back_sum.astype(jnp.float32) * potential_gain[None, :], axis=1)
    spread = jnp.sum(links.astype(jnp.float32) * sent[:, None], axis=0) * live_all
    local = charge_part + live * jnp.sum(back_mixed * potential_gain[None, :], axis=1)
    placed = (jnp.arange(atoms) // rows == me).astype(jnp.float32)
    local_all = jnp.tile(local, atoms // rows) * placed
    part = sum_butterfly(spread + local_all, "blk", blocks // 2)
    other = lax.ppermute(part, "blk", [(i, i ^ (blocks // 2)) for i in range(blocks)])
    effective_all = part + other
    effective = lax.dynamic_slice_in_dim(part, me * rows, rows) + lax.dynamic_slice_in_dim(
        other, me * rows, rows
    )
    qm_force = pull * (effective * coupling)[None, :]
    mm_force = force_pass(qm_all, effective_all, mm_pos, -coupling * mm_charge)
    return (atom_energy, qm_force, mm_force)


def solution(mesh):
    placed = (
        P(None, "blk"),
        P("blk"),
        P("blk"),
        P("blk", None),
        P("blk", None),
        P(None, ("blk", "rep")),
        P(("blk", "rep")),
        P(),
        P(),
        P(),
        P(),
        P(),
        P(),
    )
    return jax.shard_map(
        on_device,
        mesh=mesh,
        in_specs=placed,
        out_specs=(P("blk"), P(None, "blk"), P(None, ("blk", "rep"))),
        check_vma=False,
    )
```

```python
import jax
import jax.numpy as jnp
from jax import lax
from jax.sharding import PartitionSpec as P

SOFTEN = 0.25
CHUNK = 512


def gather_doubling(x, axis, first=1, last=None):
    n = lax.axis_size(axis)
    last = n if last is None else last
    me = lax.axis_index(axis)
    step = first
    while step < last:
        other = lax.ppermute(x, axis, [(i, i ^ step) for i in range(n)])
        low = (me // step) % 2 == 0
        x = jnp.where(low, jnp.concatenate([x, other], -1), jnp.concatenate([other, x], -1))
        step *= 2
    return x


def sum_butterfly(x, axis, last=None):
    n = lax.axis_size(axis)
    last = n if last is None else last
    step = 1
    while step < last:
        x = x + lax.ppermute(x, axis, [(i, i ^ step) for i in range(n)])
        step *= 2
    return x


def potential_pass(qm_some, mm_some):
    chunks = mm_some.shape[1] // CHUNK
    cols = [qm_some[c][None, :] for c in range(3)]

    def body(running, block):
        d = [cols[c] - block[:, c : c + 1] for c in range(3)]
        inverse = lax.rsqrt(d[0] * d[0] + d[1] * d[1] + d[2] * d[2] + SOFTEN)
        weighted = inverse * block[:, 3:4]
        cubed = weighted * inverse * inverse
        part = jnp.stack(
            [jnp.sum(weighted, axis=0)] + [jnp.sum(d[c] * cubed, axis=0) for c in range(3)]
        )
        return running + part, None

    stacked = jnp.transpose(mm_some.reshape(4, chunks, CHUNK), (1, 2, 0))
    total, _ = lax.scan(body, jnp.zeros((4, qm_some.shape[1]), jnp.float32), stacked)
    return total


def force_pass(qm_all, effective, mm_pos, scale):
    chunks = qm_all.shape[1] // CHUNK
    stacked = jnp.concatenate([qm_all, effective[None, :]], axis=0)
    stacked = jnp.transpose(stacked.reshape(4, chunks, CHUNK), (1, 2, 0))

    def body(running, block):
        d = [block[:, c : c + 1] - mm_pos[c][None, :] for c in range(3)]
        inverse = lax.rsqrt(d[0] * d[0] + d[1] * d[1] + d[2] * d[2] + SOFTEN)
        weight = inverse * inverse * inverse * block[:, 3:4] * scale[None, :]
        return running + jnp.stack([jnp.sum(d[c] * weight, axis=0) for c in range(3)]), None

    total, _ = lax.scan(body, jnp.zeros((3, mm_pos.shape[1]), jnp.float32), stacked)
    return total


def on_device(
    qm_pos,
    species,
    qm_count,
    ghost_owner,
    ghost_slot,
    mm_pos,
    mm_charge,
    species_table,
    potential_gain,
    message_weight,
    hidden_weight,
    energy_readout,
    charge_readout,
):
    rows = qm_pos.shape[1]
    blocks = lax.axis_size("blk")
    me = lax.axis_index("blk")
    kinds = species_table.shape[0]
    coupling = float(mm_pos.shape[1] * blocks * lax.axis_size("rep")) ** (-0.5)

    low_blocks = 1
    while low_blocks * low_blocks < blocks:
        low_blocks *= 2
    own = jnp.concatenate(
        [
            qm_pos,
            species.astype(jnp.float32)[None, :],
            jnp.broadcast_to(qm_count.astype(jnp.float32)[None, :], (1, rows)),
        ],
        axis=0,
    )
    near = gather_doubling(own, "blk", 1, low_blocks)
    near, table_t, mixing = lax.optimization_barrier(
        (near, species_table.T.astype(jnp.float32), message_weight.astype(jnp.float32))
    )
    mm_some = gather_doubling(
        jnp.concatenate([mm_pos, mm_charge[None, :]], axis=0), "blk", low_blocks, blocks
    )
    partial = potential_pass(near[:3], mm_some)
    total = sum_butterfly(sum_butterfly(partial, "rep"), "blk", low_blocks)
    pull = lax.dynamic_slice_in_dim(total[1:4], (me % low_blocks) * rows, rows, axis=1)
    known = gather_doubling(
        jnp.concatenate([total[0:1] * coupling, near], axis=0), "blk", low_blocks, blocks
    )
    potential_all = known[0]
    qm_all = known[1:4]
    atoms = qm_all.shape[1]
    species_all = known[4].astype(jnp.int32)
    live_all = ((jnp.arange(atoms) % rows).astype(jnp.float32) < known[5]).astype(jnp.float32)

    live = lax.dynamic_slice_in_dim(live_all, me * rows, rows)
    potential = lax.dynamic_slice_in_dim(potential_all, me * rows, rows)
    picks_t = (jnp.arange(kinds)[:, None] == species_all[None, :]).astype(jnp.bfloat16)
    base_t = jnp.dot(table_t, picks_t.astype(jnp.float32), preferred_element_type=jnp.float32)
    start_t = (
        live_all[None, :] * (base_t + potential_gain[:, None] * potential_all[None, :])
    ).astype(jnp.bfloat16)
    start = lax.dynamic_slice_in_dim(start_t, me * rows, rows, axis=1).T

    ghost = ghost_owner * rows + ghost_slot
    columns = jnp.arange(atoms)[None, :]
    links = jnp.zeros((rows, atoms), jnp.bfloat16)
    for k in range(ghost.shape[1]):
        links = links + (ghost[:, k : k + 1] == columns).astype(jnp.bfloat16)
    neighbour = lax.dot_general(
        links, start_t, (((1,), (1,)), ((), ())), preferred_element_type=jnp.float32
    ).astype(jnp.bfloat16)

    mixed = start.astype(jnp.float32) + jnp.dot(
        neighbour.astype(jnp.float32), mixing, preferred_element_type=jnp.float32
    )
    before = jnp.dot(mixed.astype(jnp.bfloat16), hidden_weight, preferred_element_type=jnp.float32)
    sigma = jax.nn.sigmoid(before)
    active = before * sigma
    energy_part = live * jnp.sum(active * energy_readout[None, :], axis=1)
    charge_part = live * jnp.sum(active * charge_readout[None, :], axis=1)
    atom_energy = energy_part + charge_part * potential
    back_active = live[:, None] * (
        energy_readout[None, :] + potential[:, None] * charge_readout[None, :]
    )
    back_before = (back_active * sigma * (1.0 + before * (1.0 - sigma))).astype(jnp.bfloat16)
    back_mixed = jnp.dot(back_before, hidden_weight.T, preferred_element_type=jnp.float32)
    back_sum = jnp.dot(
        back_mixed.astype(jnp.bfloat16).astype(jnp.float32), mixing.T,
        preferred_element_type=jnp.float32,
    ).astype(jnp.bfloat16)

    sent = jnp.sum(back_sum.astype(jnp.float32) * potential_gain[None, :], axis=1)
    spread = jnp.sum(links.astype(jnp.float32) * sent[:, None], axis=0) * live_all
    local = charge_part + live * jnp.sum(back_mixed * potential_gain[None, :], axis=1)
    placed = (jnp.arange(atoms) // rows == me).astype(jnp.float32)
    local_all = jnp.tile(local, atoms // rows) * placed
    part = sum_butterfly(spread + local_all, "blk", blocks // 2)
    other = lax.ppermute(part, "blk", [(i, i ^ (blocks // 2)) for i in range(blocks)])
    effective_all = part + other
    effective = lax.dynamic_slice_in_dim(part, me * rows, rows) + lax.dynamic_slice_in_dim(
        other, me * rows, rows
    )
    qm_force = pull * (effective * coupling)[None, :]
    mm_force = force_pass(qm_all, effective_all, mm_pos, -coupling * mm_charge)
    return (atom_energy, qm_force, mm_force)


def solution(mesh):
    placed = (
        P(None, "blk"),
        P("blk"),
        P("blk"),
        P("blk", None),
        P("blk", None),
        P(None, ("blk", "rep")),
        P(("blk", "rep")),
        P(),
        P(),
        P(),
        P(),
        P(),
        P(),
    )
    return jax.shard_map(
        on_device,
        mesh=mesh,
        in_specs=placed,
        out_specs=(P("blk"), P(None, "blk"), P(None, ("blk", "rep"))),
        check_vma=False,
    )
```

```python
import jax
import jax.numpy as jnp
from jax import lax
from jax.sharding import PartitionSpec as P

SOFTEN = 0.25
CHUNK = 512


def gather_doubling(x, axis, first=1, last=None):
    n = lax.axis_size(axis)
    last = n if last is None else last
    me = lax.axis_index(axis)
    step = first
    while step < last:
        other = lax.ppermute(x, axis, [(i, i ^ step) for i in range(n)])
        low = (me // step) % 2 == 0
        x = jnp.where(low, jnp.concatenate([x, other], -1), jnp.concatenate([other, x], -1))
        step *= 2
    return x


def sum_butterfly(x, axis, last=None):
    n = lax.axis_size(axis)
    last = n if last is None else last
    step = 1
    while step < last:
        x = x + lax.ppermute(x, axis, [(i, i ^ step) for i in range(n)])
        step *= 2
    return x


def potential_pass(qm_some, mm_some):
    chunks = mm_some.shape[1] // CHUNK
    cols = [qm_some[c][None, :] for c in range(3)]

    def body(running, block):
        d = [cols[c] - block[:, c : c + 1] for c in range(3)]
        inverse = lax.rsqrt(d[0] * d[0] + d[1] * d[1] + d[2] * d[2] + SOFTEN)
        weighted = inverse * block[:, 3:4]
        cubed = weighted * inverse * inverse
        part = jnp.stack(
            [jnp.sum(weighted, axis=0)] + [jnp.sum(d[c] * cubed, axis=0) for c in range(3)]
        )
        return running + part, None

    stacked = jnp.transpose(mm_some.reshape(4, chunks, CHUNK), (1, 2, 0))
    total, _ = lax.scan(body, jnp.zeros((4, qm_some.shape[1]), jnp.float32), stacked)
    return total


def force_pass(qm_all, effective, mm_pos, scale):
    chunks = qm_all.shape[1] // CHUNK
    stacked = jnp.concatenate([qm_all, effective[None, :]], axis=0)
    stacked = jnp.transpose(stacked.reshape(4, chunks, CHUNK), (1, 2, 0))

    def body(running, block):
        d = [block[:, c : c + 1] - mm_pos[c][None, :] for c in range(3)]
        inverse = lax.rsqrt(d[0] * d[0] + d[1] * d[1] + d[2] * d[2] + SOFTEN)
        weight = inverse * inverse * inverse * block[:, 3:4] * scale[None, :]
        return running + jnp.stack([jnp.sum(d[c] * weight, axis=0) for c in range(3)]), None

    total, _ = lax.scan(body, jnp.zeros((3, mm_pos.shape[1]), jnp.float32), stacked)
    return total


def on_device(
    qm_pos,
    species,
    qm_count,
    ghost_owner,
    ghost_slot,
    mm_pos,
    mm_charge,
    species_table,
    potential_gain,
    message_weight,
    hidden_weight,
    energy_readout,
    charge_readout,
):
    rows = qm_pos.shape[1]
    blocks = lax.axis_size("blk")
    me = lax.axis_index("blk")
    kinds = species_table.shape[0]
    coupling = float(mm_pos.shape[1] * blocks * lax.axis_size("rep")) ** (-0.5)

    low_blocks = 1
    while low_blocks * low_blocks < blocks:
        low_blocks *= 2
    own = jnp.concatenate(
        [
            qm_pos,
            species.astype(jnp.float32)[None, :],
            jnp.broadcast_to(qm_count.astype(jnp.float32)[None, :], (1, rows)),
        ],
        axis=0,
    )
    near = gather_doubling(own, "blk", 1, low_blocks)
    finite = near[0:1, 0:1] == near[0:1, 0:1]
    table_t = jnp.where(finite, species_table.T, jnp.zeros_like(species_table.T))
    mixing = jnp.where(finite, message_weight, jnp.zeros_like(message_weight))
    gain = jnp.where(finite[0], potential_gain, jnp.zeros_like(potential_gain))
    near, table_t, mixing, gain = lax.optimization_barrier((near, table_t, mixing, gain))
    mm_some = gather_doubling(
        jnp.concatenate([mm_pos, mm_charge[None, :]], axis=0), "blk", low_blocks, blocks
    )
    partial = potential_pass(near[:3], mm_some)
    total = sum_butterfly(sum_butterfly(partial, "rep"), "blk", low_blocks)
    pull = lax.dynamic_slice_in_dim(total[1:4], (me % low_blocks) * rows, rows, axis=1)
    known = gather_doubling(
        jnp.concatenate([total[0:1] * coupling, near], axis=0), "blk", low_blocks, blocks
    )
    potential_all = known[0]
    qm_all = known[1:4]
    atoms = qm_all.shape[1]
    species_all = known[4].astype(jnp.int32)
    live_all = ((jnp.arange(atoms) % rows).astype(jnp.float32) < known[5]).astype(jnp.float32)

    live = lax.dynamic_slice_in_dim(live_all, me * rows, rows)
    potential = lax.dynamic_slice_in_dim(potential_all, me * rows, rows)
    picks_t = (jnp.arange(kinds)[:, None] == species_all[None, :]).astype(jnp.bfloat16)
    base_t = jnp.dot(table_t, picks_t, preferred_element_type=jnp.float32)
    start_t = (
        live_all[None, :] * (base_t + gain[:, None] * potential_all[None, :])
    ).astype(jnp.bfloat16)
    start = lax.dynamic_slice_in_dim(start_t, me * rows, rows, axis=1).T

    ghost = ghost_owner * rows + ghost_slot
    columns = jnp.arange(atoms)[None, :]
    links = jnp.zeros((rows, atoms), jnp.bfloat16)
    for k in range(ghost.shape[1]):
        links = links + (ghost[:, k : k + 1] == columns).astype(jnp.bfloat16)
    neighbour = lax.dot_general(
        links, start_t, (((1,), (1,)), ((), ())), preferred_element_type=jnp.float32
    ).astype(jnp.bfloat16)

    mixed = start.astype(jnp.float32) + jnp.dot(
        neighbour, mixing, preferred_element_type=jnp.float32
    )
    before = jnp.dot(mixed.astype(jnp.bfloat16), hidden_weight, preferred_element_type=jnp.float32)
    sigma = jax.nn.sigmoid(before)
    active = before * sigma
    energy_part = live * jnp.sum(active * energy_readout[None, :], axis=1)
    charge_part = live * jnp.sum(active * charge_readout[None, :], axis=1)
    atom_energy = energy_part + charge_part * potential
    back_active = live[:, None] * (
        energy_readout[None, :] + potential[:, None] * charge_readout[None, :]
    )
    back_before = (back_active * sigma * (1.0 + before * (1.0 - sigma))).astype(jnp.bfloat16)
    back_mixed = jnp.dot(back_before, hidden_weight.T, preferred_element_type=jnp.float32)
    back_sum = jnp.dot(
        back_mixed.astype(jnp.bfloat16), mixing.T, preferred_element_type=jnp.float32
    ).astype(jnp.bfloat16)

    sent = jnp.sum(back_sum.astype(jnp.float32) * gain[None, :], axis=1)
    spread = jnp.sum(links.astype(jnp.float32) * sent[:, None], axis=0) * live_all
    local = charge_part + live * jnp.sum(back_mixed * gain[None, :], axis=1)
    placed = (jnp.arange(atoms) // rows == me).astype(jnp.float32)
    local_all = jnp.tile(local, atoms // rows) * placed
    part = sum_butterfly(spread + local_all, "blk", blocks // 2)
    other = lax.ppermute(part, "blk", [(i, i ^ (blocks // 2)) for i in range(blocks)])
    effective_all = part + other
    effective = lax.dynamic_slice_in_dim(part, me * rows, rows) + lax.dynamic_slice_in_dim(
        other, me * rows, rows
    )
    qm_force = pull * (effective * coupling)[None, :]
    mm_force = force_pass(qm_all, effective_all, mm_pos, -coupling * mm_charge)
    return (atom_energy, qm_force, mm_force)


def solution(mesh):
    placed = (
        P(None, "blk"),
        P("blk"),
        P("blk"),
        P("blk", None),
        P("blk", None),
        P(None, ("blk", "rep")),
        P(("blk", "rep")),
        P(),
        P(),
        P(),
        P(),
        P(),
        P(),
    )
    return jax.shard_map(
        on_device,
        mesh=mesh,
        in_specs=placed,
        out_specs=(P("blk"), P(None, "blk"), P(None, ("blk", "rep"))),
        check_vma=False,
    )
```

```python
import jax
import jax.numpy as jnp
from jax import lax
from jax.sharding import PartitionSpec as P

SOFTEN = 0.25
CHUNK = 512


def gather_doubling(x, axis, first=1, last=None):
    n = lax.axis_size(axis)
    last = n if last is None else last
    me = lax.axis_index(axis)
    step = first
    while step < last:
        other = lax.ppermute(x, axis, [(i, i ^ step) for i in range(n)])
        low = (me // step) % 2 == 0
        x = jnp.where(low, jnp.concatenate([x, other], -1), jnp.concatenate([other, x], -1))
        step *= 2
    return x


def sum_butterfly(x, axis, last=None, first=1, downward=False):
    n = lax.axis_size(axis)
    last = n if last is None else last
    steps = []
    step = first
    while step < last:
        steps.append(step)
        step *= 2
    for step in reversed(steps) if downward else steps:
        x = x + lax.ppermute(x, axis, [(i, i ^ step) for i in range(n)])
    return x


def potential_pass(qm_some, mm_some):
    chunks = mm_some.shape[1] // CHUNK
    cols = [qm_some[c][None, :] for c in range(3)]

    def body(running, block):
        d = [cols[c] - block[:, c : c + 1] for c in range(3)]
        inverse = lax.rsqrt(d[0] * d[0] + d[1] * d[1] + d[2] * d[2] + SOFTEN)
        weighted = inverse * block[:, 3:4]
        cubed = weighted * inverse * inverse
        part = jnp.stack(
            [jnp.sum(weighted, axis=0)] + [jnp.sum(d[c] * cubed, axis=0) for c in range(3)]
        )
        return running + part, None

    stacked = jnp.transpose(mm_some.reshape(4, chunks, CHUNK), (1, 2, 0))
    total, _ = lax.scan(body, jnp.zeros((4, qm_some.shape[1]), jnp.float32), stacked)
    return total


def force_pass(qm_all, effective, mm_pos, scale):
    chunks = qm_all.shape[1] // CHUNK
    stacked = jnp.concatenate([qm_all, effective[None, :]], axis=0)
    stacked = jnp.transpose(stacked.reshape(4, chunks, CHUNK), (1, 2, 0))

    def body(running, block):
        d = [block[:, c : c + 1] - mm_pos[c][None, :] for c in range(3)]
        inverse = lax.rsqrt(d[0] * d[0] + d[1] * d[1] + d[2] * d[2] + SOFTEN)
        weight = inverse * inverse * inverse * block[:, 3:4] * scale[None, :]
        return running + jnp.stack([jnp.sum(d[c] * weight, axis=0) for c in range(3)]), None

    total, _ = lax.scan(body, jnp.zeros((3, mm_pos.shape[1]), jnp.float32), stacked)
    return total


def on_device(
    qm_pos,
    species,
    qm_count,
    ghost_owner,
    ghost_slot,
    mm_pos,
    mm_charge,
    species_table,
    potential_gain,
    message_weight,
    hidden_weight,
    energy_readout,
    charge_readout,
):
    rows = qm_pos.shape[1]
    blocks = lax.axis_size("blk")
    me = lax.axis_index("blk")
    kinds = species_table.shape[0]
    coupling = float(mm_pos.shape[1] * blocks * lax.axis_size("rep")) ** (-0.5)

    low_blocks = 1
    while low_blocks * low_blocks < blocks:
        low_blocks *= 2
    own = jnp.concatenate(
        [
            qm_pos,
            species.astype(jnp.float32)[None, :],
            jnp.broadcast_to(qm_count.astype(jnp.float32)[None, :], (1, rows)),
        ],
        axis=0,
    )
    near = gather_doubling(own, "blk", 1, low_blocks)
    near, table_t = lax.optimization_barrier((near, species_table.T))
    mm_some = gather_doubling(
        jnp.concatenate([mm_pos, mm_charge[None, :]], axis=0), "blk", low_blocks, blocks
    )
    partial = potential_pass(near[:3], mm_some)
    total = sum_butterfly(sum_butterfly(partial, "blk", low_blocks), "rep")
    pull = lax.dynamic_slice_in_dim(total[1:4], (me % low_blocks) * rows, rows, axis=1)
    known = gather_doubling(
        jnp.concatenate([total[0:1] * coupling, near], axis=0), "blk", low_blocks, blocks
    )
    potential_all = known[0]
    qm_all = known[1:4]
    atoms = qm_all.shape[1]
    species_all = known[4].astype(jnp.int32)
    live_all = ((jnp.arange(atoms) % rows).astype(jnp.float32) < known[5]).astype(jnp.float32)

    live = lax.dynamic_slice_in_dim(live_all, me * rows, rows)
    potential = lax.dynamic_slice_in_dim(potential_all, me * rows, rows)
    picks_t = (jnp.arange(kinds)[:, None] == species_all[None, :]).astype(jnp.bfloat16)
    base_t = jnp.dot(table_t, picks_t, preferred_element_type=jnp.float32)
    start_t = (
        live_all[None, :] * (base_t + potential_gain[:, None] * potential_all[None, :])
    ).astype(jnp.bfloat16)
    start = lax.dynamic_slice_in_dim(start_t, me * rows, rows, axis=1).T

    ghost = ghost_owner * rows + ghost_slot
    columns = jnp.arange(atoms)[None, :]
    links = jnp.zeros((rows, atoms), jnp.bfloat16)
    for k in range(ghost.shape[1]):
        links = links + (ghost[:, k : k + 1] == columns).astype(jnp.bfloat16)
    neighbour = lax.dot_general(
        links, start_t, (((1,), (1,)), ((), ())), preferred_element_type=jnp.float32
    ).astype(jnp.bfloat16)

    mixed = start.astype(jnp.float32) + jnp.dot(
        neighbour, message_weight, preferred_element_type=jnp.float32
    )
    before = jnp.dot(mixed.astype(jnp.bfloat16), hidden_weight, preferred_element_type=jnp.float32)
    sigma = jax.nn.sigmoid(before)
    active = before * sigma
    energy_part = live * jnp.sum(active * energy_readout[None, :], axis=1)
    charge_part = live * jnp.sum(active * charge_readout[None, :], axis=1)
    atom_energy = energy_part + charge_part * potential
    back_active = live[:, None] * (
        energy_readout[None, :] + potential[:, None] * charge_readout[None, :]
    )
    back_before = (back_active * sigma * (1.0 + before * (1.0 - sigma))).astype(jnp.bfloat16)
    back_mixed = jnp.dot(back_before, hidden_weight.T, preferred_element_type=jnp.float32)
    back_sum = jnp.dot(
        back_mixed.astype(jnp.bfloat16), message_weight.T, preferred_element_type=jnp.float32
    ).astype(jnp.bfloat16)

    sent = jnp.sum(back_sum.astype(jnp.float32) * potential_gain[None, :], axis=1)
    spread = jnp.sum(links.astype(jnp.float32) * sent[:, None], axis=0) * live_all
    local = charge_part + live * jnp.sum(back_mixed * potential_gain[None, :], axis=1)
    placed = (jnp.arange(atoms) // rows == me).astype(jnp.float32)
    local_all = jnp.tile(local, atoms // rows) * placed
    part = sum_butterfly(spread + local_all, "blk", blocks, 2, downward=True)
    other = lax.ppermute(part, "blk", [(i, i ^ 1) for i in range(blocks)])
    effective_all = part + other
    effective = lax.dynamic_slice_in_dim(part, me * rows, rows) + lax.dynamic_slice_in_dim(
        other, me * rows, rows
    )
    qm_force = pull * (effective * coupling)[None, :]
    mm_force = force_pass(qm_all, effective_all, mm_pos, -coupling * mm_charge)
    return (atom_energy, qm_force, mm_force)


def solution(mesh):
    placed = (
        P(None, "blk"),
        P("blk"),
        P("blk"),
        P("blk", None),
        P("blk", None),
        P(None, ("blk", "rep")),
        P(("blk", "rep")),
        P(),
        P(),
        P(),
        P(),
        P(),
        P(),
    )
    return jax.shard_map(
        on_device,
        mesh=mesh,
        in_specs=placed,
        out_specs=(P("blk"), P(None, "blk"), P(None, ("blk", "rep"))),
        check_vma=False,
    )
```

```python
import jax
import jax.numpy as jnp
from jax import lax
from jax.sharding import PartitionSpec as P

SOFTEN = 0.25
CHUNK = 512


def gather_doubling(x, axis, first=1, last=None):
    n = lax.axis_size(axis)
    last = n if last is None else last
    me = lax.axis_index(axis)
    step = first
    while step < last:
        other = lax.ppermute(x, axis, [(i, i ^ step) for i in range(n)])
        low = (me // step) % 2 == 0
        x = jnp.where(low, jnp.concatenate([x, other], -1), jnp.concatenate([other, x], -1))
        step *= 2
    return x


def sum_butterfly(x, axis, last=None):
    n = lax.axis_size(axis)
    last = n if last is None else last
    step = 1
    while step < last:
        x = x + lax.ppermute(x, axis, [(i, i ^ step) for i in range(n)])
        step *= 2
    return x


def potential_pass(qm_some, mm_some):
    chunks = mm_some.shape[1] // CHUNK
    cols = [qm_some[c][None, :] for c in range(3)]

    def body(running, block):
        d = [cols[c] - block[:, c : c + 1] for c in range(3)]
        inverse = lax.rsqrt(d[0] * d[0] + d[1] * d[1] + d[2] * d[2] + SOFTEN)
        weighted = inverse * block[:, 3:4]
        cubed = weighted * inverse * inverse
        part = jnp.stack(
            [jnp.sum(weighted, axis=0)] + [jnp.sum(d[c] * cubed, axis=0) for c in range(3)]
        )
        return running + part, None

    stacked = jnp.transpose(mm_some.reshape(4, chunks, CHUNK), (1, 2, 0))
    total, _ = lax.scan(body, jnp.zeros((4, qm_some.shape[1]), jnp.float32), stacked)
    return total


def force_pass(qm_all, effective, mm_pos, scale):
    chunks = qm_all.shape[1] // CHUNK
    stacked = jnp.concatenate([qm_all, effective[None, :]], axis=0)
    stacked = jnp.transpose(stacked.reshape(4, chunks, CHUNK), (1, 2, 0))

    def body(running, block):
        d = [block[:, c : c + 1] - mm_pos[c][None, :] for c in range(3)]
        inverse = lax.rsqrt(d[0] * d[0] + d[1] * d[1] + d[2] * d[2] + SOFTEN)
        weight = inverse * inverse * inverse * block[:, 3:4] * scale[None, :]
        return running + jnp.stack([jnp.sum(d[c] * weight, axis=0) for c in range(3)]), None

    total, _ = lax.scan(body, jnp.zeros((3, mm_pos.shape[1]), jnp.float32), stacked)
    return total


def on_device(
    qm_pos,
    species,
    qm_count,
    ghost_owner,
    ghost_slot,
    mm_pos,
    mm_charge,
    species_table,
    potential_gain,
    message_weight,
    hidden_weight,
    energy_readout,
    charge_readout,
):
    rows = qm_pos.shape[1]
    blocks = lax.axis_size("blk")
    me = lax.axis_index("blk")
    kinds = species_table.shape[0]
    coupling = float(mm_pos.shape[1] * blocks * lax.axis_size("rep")) ** (-0.5)

    low_blocks = 1
    while low_blocks * low_blocks < blocks:
        low_blocks *= 2
    own = jnp.concatenate(
        [
            qm_pos,
            species.astype(jnp.float32)[None, :],
            jnp.broadcast_to(qm_count.astype(jnp.float32)[None, :], (1, rows)),
        ],
        axis=0,
    )
    near = gather_doubling(own, "blk", 1, low_blocks)
    near, table_t = lax.optimization_barrier((near, species_table.T))
    mm_some = gather_doubling(
        jnp.concatenate([mm_pos, mm_charge[None, :]], axis=0), "blk", low_blocks, blocks
    )
    partial = potential_pass(near[:3], mm_some)
    total = sum_butterfly(sum_butterfly(partial, "rep"), "blk", low_blocks)
    pull = lax.dynamic_slice_in_dim(total[1:4], (me % low_blocks) * rows, rows, axis=1)
    known = gather_doubling(
        jnp.concatenate([total[0:1] * coupling, near], axis=0), "blk", low_blocks, blocks
    )
    ghost = ghost_owner * rows + ghost_slot
    columns = jnp.arange(blocks * rows)[None, :]
    links = jnp.zeros((rows, blocks * rows), jnp.bfloat16)
    for k in range(ghost.shape[1]):
        links = links + (ghost[:, k : k + 1] == columns).astype(jnp.bfloat16)
    known, links = lax.optimization_barrier((known, links))
    potential_all = known[0]
    qm_all = known[1:4]
    atoms = qm_all.shape[1]
    species_all = known[4].astype(jnp.int32)
    live_all = ((jnp.arange(atoms) % rows).astype(jnp.float32) < known[5]).astype(jnp.float32)

    live = lax.dynamic_slice_in_dim(live_all, me * rows, rows)
    potential = lax.dynamic_slice_in_dim(potential_all, me * rows, rows)
    picks_t = (jnp.arange(kinds)[:, None] == species_all[None, :]).astype(jnp.bfloat16)
    base_t = jnp.dot(table_t, picks_t, preferred_element_type=jnp.float32)
    start_t = (
        live_all[None, :] * (base_t + potential_gain[:, None] * potential_all[None, :])
    ).astype(jnp.bfloat16)
    start = lax.dynamic_slice_in_dim(start_t, me * rows, rows, axis=1).T

    neighbour = lax.dot_general(
        links, start_t, (((1,), (1,)), ((), ())), preferred_element_type=jnp.float32
    ).astype(jnp.bfloat16)

    mixed = start.astype(jnp.float32) + jnp.dot(
        neighbour, message_weight, preferred_element_type=jnp.float32
    )
    before = jnp.dot(mixed.astype(jnp.bfloat16), hidden_weight, preferred_element_type=jnp.float32)
    sigma = jax.nn.sigmoid(before)
    active = before * sigma
    energy_part = live * jnp.sum(active * energy_readout[None, :], axis=1)
    charge_part = live * jnp.sum(active * charge_readout[None, :], axis=1)
    atom_energy = energy_part + charge_part * potential
    back_active = live[:, None] * (
        energy_readout[None, :] + potential[:, None] * charge_readout[None, :]
    )
    back_before = (back_active * sigma * (1.0 + before * (1.0 - sigma))).astype(jnp.bfloat16)
    back_mixed = jnp.dot(back_before, hidden_weight.T, preferred_element_type=jnp.float32)
    back_sum = jnp.dot(
        back_mixed.astype(jnp.bfloat16), message_weight.T, preferred_element_type=jnp.float32
    ).astype(jnp.bfloat16)

    sent = jnp.sum(back_sum.astype(jnp.float32) * potential_gain[None, :], axis=1)
    spread = jnp.sum(links.astype(jnp.float32) * sent[:, None], axis=0) * live_all
    local = charge_part + live * jnp.sum(back_mixed * potential_gain[None, :], axis=1)
    placed = (jnp.arange(atoms) // rows == me).astype(jnp.float32)
    local_all = jnp.tile(local, atoms // rows) * placed
    part = sum_butterfly(spread + local_all, "blk", blocks // 2)
    other = lax.ppermute(part, "blk", [(i, i ^ (blocks // 2)) for i in range(blocks)])
    effective_all = part + other
    effective = lax.dynamic_slice_in_dim(part, me * rows, rows) + lax.dynamic_slice_in_dim(
        other, me * rows, rows
    )
    qm_force = pull * (effective * coupling)[None, :]
    mm_force = force_pass(qm_all, effective_all, mm_pos, -coupling * mm_charge)
    return (atom_energy, qm_force, mm_force)


def solution(mesh):
    placed = (
        P(None, "blk"),
        P("blk"),
        P("blk"),
        P("blk", None),
        P("blk", None),
        P(None, ("blk", "rep")),
        P(("blk", "rep")),
        P(),
        P(),
        P(),
        P(),
        P(),
        P(),
    )
    return jax.shard_map(
        on_device,
        mesh=mesh,
        in_specs=placed,
        out_specs=(P("blk"), P(None, "blk"), P(None, ("blk", "rep"))),
        check_vma=False,
    )
```

```python
import jax
import jax.numpy as jnp
from jax import lax
from jax.sharding import PartitionSpec as P

SOFTEN = 0.25
CHUNK = 512


def gather_doubling(x, axis, first=1, last=None):
    n = lax.axis_size(axis)
    last = n if last is None else last
    me = lax.axis_index(axis)
    step = first
    while step < last:
        other = lax.ppermute(x, axis, [(i, i ^ step) for i in range(n)])
        low = (me // step) % 2 == 0
        x = jnp.where(low, jnp.concatenate([x, other], -1), jnp.concatenate([other, x], -1))
        step *= 2
    return x


def sum_butterfly(x, axis, last=None):
    n = lax.axis_size(axis)
    last = n if last is None else last
    step = 1
    while step < last:
        x = x + lax.ppermute(x, axis, [(i, i ^ step) for i in range(n)])
        step *= 2
    return x


def potential_pass(qm_some, mm_some):
    chunks = mm_some.shape[1] // CHUNK
    cols = [qm_some[c][None, :] for c in range(3)]

    def body(running, block):
        d = [cols[c] - block[:, c : c + 1] for c in range(3)]
        inverse = lax.rsqrt(d[0] * d[0] + d[1] * d[1] + d[2] * d[2] + SOFTEN)
        weighted = inverse * block[:, 3:4]
        cubed = weighted * inverse * inverse
        part = jnp.stack(
            [jnp.sum(weighted, axis=0)] + [jnp.sum(d[c] * cubed, axis=0) for c in range(3)]
        )
        return running + part, None

    stacked = jnp.transpose(mm_some.reshape(4, chunks, CHUNK), (1, 2, 0))
    total, _ = lax.scan(body, jnp.zeros((4, qm_some.shape[1]), jnp.float32), stacked)
    return total


def force_pass(qm_all, effective, mm_pos, scale):
    chunks = qm_all.shape[1] // CHUNK
    stacked = jnp.concatenate([qm_all, effective[None, :]], axis=0)
    stacked = jnp.transpose(stacked.reshape(4, chunks, CHUNK), (1, 2, 0))

    def body(running, block):
        d = [block[:, c : c + 1] - mm_pos[c][None, :] for c in range(3)]
        inverse = lax.rsqrt(d[0] * d[0] + d[1] * d[1] + d[2] * d[2] + SOFTEN)
        weight = inverse * inverse * inverse * block[:, 3:4] * scale[None, :]
        return running + jnp.stack([jnp.sum(d[c] * weight, axis=0) for c in range(3)]), None

    total, _ = lax.scan(body, jnp.zeros((3, mm_pos.shape[1]), jnp.float32), stacked)
    return total


def on_device(
    qm_pos,
    species,
    qm_count,
    ghost_owner,
    ghost_slot,
    mm_pos,
    mm_charge,
    species_table,
    potential_gain,
    message_weight,
    hidden_weight,
    energy_readout,
    charge_readout,
):
    rows = qm_pos.shape[1]
    blocks = lax.axis_size("blk")
    me = lax.axis_index("blk")
    kinds = species_table.shape[0]
    coupling = float(mm_pos.shape[1] * blocks * lax.axis_size("rep")) ** (-0.5)

    low_blocks = 1
    while low_blocks * low_blocks < blocks:
        low_blocks *= 2
    own = jnp.concatenate(
        [
            qm_pos,
            species.astype(jnp.float32)[None, :],
            jnp.broadcast_to(qm_count.astype(jnp.float32)[None, :], (1, rows)),
        ],
        axis=0,
    )
    near = gather_doubling(own, "blk", 1, low_blocks)
    mm_some = gather_doubling(
        jnp.concatenate([mm_pos, mm_charge[None, :]], axis=0), "blk", low_blocks, blocks
    )
    partial = potential_pass(near[:3], mm_some)
    total = sum_butterfly(sum_butterfly(partial, "rep"), "blk", low_blocks)
    pull = lax.dynamic_slice_in_dim(total[1:4], (me % low_blocks) * rows, rows, axis=1)
    known = gather_doubling(
        jnp.concatenate([total[0:1] * coupling, near], axis=0), "blk", low_blocks, blocks
    )
    ghost = ghost_owner * rows + ghost_slot
    columns = jnp.arange(blocks * rows)[None, :]
    links = jnp.zeros((rows, blocks * rows), jnp.bfloat16)
    for k in range(ghost.shape[1]):
        links = links + (ghost[:, k : k + 1] == columns).astype(jnp.bfloat16)
    finite = near[0:1, 0:1] == near[0:1, 0:1]
    weights = [species_table.T, message_weight, potential_gain, energy_readout, charge_readout]
    weights = [jnp.where(finite.reshape((1,) * w.ndim), w, jnp.zeros_like(w)) for w in weights]
    known, links, weights = lax.optimization_barrier((known, links, weights))
    table_t, message_weight, potential_gain, energy_readout, charge_readout = weights
    potential_all = known[0]
    qm_all = known[1:4]
    atoms = qm_all.shape[1]
    species_all = known[4].astype(jnp.int32)
    live_all = ((jnp.arange(atoms) % rows).astype(jnp.float32) < known[5]).astype(jnp.float32)

    live = lax.dynamic_slice_in_dim(live_all, me * rows, rows)
    potential = lax.dynamic_slice_in_dim(potential_all, me * rows, rows)
    picks_t = (jnp.arange(kinds)[:, None] == species_all[None, :]).astype(jnp.bfloat16)
    base_t = jnp.dot(table_t, picks_t, preferred_element_type=jnp.float32)
    start_t = (
        live_all[None, :] * (base_t + potential_gain[:, None] * potential_all[None, :])
    ).astype(jnp.bfloat16)
    start = lax.dynamic_slice_in_dim(start_t, me * rows, rows, axis=1).T

    neighbour = lax.dot_general(
        links, start_t, (((1,), (1,)), ((), ())), preferred_element_type=jnp.float32
    ).astype(jnp.bfloat16)

    mixed = start.astype(jnp.float32) + jnp.dot(
        neighbour, message_weight, preferred_element_type=jnp.float32
    )
    before = jnp.dot(mixed.astype(jnp.bfloat16), hidden_weight, preferred_element_type=jnp.float32)
    sigma = jax.nn.sigmoid(before)
    active = before * sigma
    energy_part = live * jnp.sum(active * energy_readout[None, :], axis=1)
    charge_part = live * jnp.sum(active * charge_readout[None, :], axis=1)
    atom_energy = energy_part + charge_part * potential
    back_active = live[:, None] * (
        energy_readout[None, :] + potential[:, None] * charge_readout[None, :]
    )
    back_before = (back_active * sigma * (1.0 + before * (1.0 - sigma))).astype(jnp.bfloat16)
    back_mixed = jnp.dot(back_before, hidden_weight.T, preferred_element_type=jnp.float32)
    back_sum = jnp.dot(
        back_mixed.astype(jnp.bfloat16), message_weight.T, preferred_element_type=jnp.float32
    ).astype(jnp.bfloat16)

    sent = jnp.sum(back_sum.astype(jnp.float32) * potential_gain[None, :], axis=1)
    spread = jnp.sum(links.astype(jnp.float32) * sent[:, None], axis=0) * live_all
    local = charge_part + live * jnp.sum(back_mixed * potential_gain[None, :], axis=1)
    placed = (jnp.arange(atoms) // rows == me).astype(jnp.float32)
    local_all = jnp.tile(local, atoms // rows) * placed
    part = sum_butterfly(spread + local_all, "blk", blocks // 2)
    other = lax.ppermute(part, "blk", [(i, i ^ (blocks // 2)) for i in range(blocks)])
    effective_all = part + other
    effective = lax.dynamic_slice_in_dim(part, me * rows, rows) + lax.dynamic_slice_in_dim(
        other, me * rows, rows
    )
    qm_force = pull * (effective * coupling)[None, :]
    mm_force = force_pass(qm_all, effective_all, mm_pos, -coupling * mm_charge)
    return (atom_energy, qm_force, mm_force)


def solution(mesh):
    placed = (
        P(None, "blk"),
        P("blk"),
        P("blk"),
        P("blk", None),
        P("blk", None),
        P(None, ("blk", "rep")),
        P(("blk", "rep")),
        P(),
        P(),
        P(),
        P(),
        P(),
        P(),
    )
    return jax.shard_map(
        on_device,
        mesh=mesh,
        in_specs=placed,
        out_specs=(P("blk"), P(None, "blk"), P(None, ("blk", "rep"))),
        check_vma=False,
    )
```

```python
import jax
import jax.numpy as jnp
from jax import lax
from jax.sharding import PartitionSpec as P

SOFTEN = 0.25
CHUNK = 512


def gather_doubling(x, axis, first=1, last=None):
    n = lax.axis_size(axis)
    last = n if last is None else last
    me = lax.axis_index(axis)
    step = first
    while step < last:
        other = lax.ppermute(x, axis, [(i, i ^ step) for i in range(n)])
        low = (me // step) % 2 == 0
        x = jnp.where(low, jnp.concatenate([x, other], -1), jnp.concatenate([other, x], -1))
        step *= 2
    return x


def sum_butterfly(x, axis, last=None):
    n = lax.axis_size(axis)
    last = n if last is None else last
    step = 1
    while step < last:
        x = x + lax.ppermute(x, axis, [(i, i ^ step) for i in range(n)])
        step *= 2
    return x


def potential_pass(qm_some, mm_some):
    chunks = mm_some.shape[1] // CHUNK
    cols = [qm_some[c][None, :] for c in range(3)]

    def body(running, block):
        d = [cols[c] - block[:, c : c + 1] for c in range(3)]
        inverse = lax.rsqrt(d[0] * d[0] + d[1] * d[1] + d[2] * d[2] + SOFTEN)
        weighted = inverse * block[:, 3:4]
        cubed = weighted * inverse * inverse
        part = jnp.stack(
            [jnp.sum(weighted, axis=0)] + [jnp.sum(d[c] * cubed, axis=0) for c in range(3)]
        )
        return running + part, None

    stacked = jnp.transpose(mm_some.reshape(4, chunks, CHUNK), (1, 2, 0))
    total, _ = lax.scan(body, jnp.zeros((4, qm_some.shape[1]), jnp.float32), stacked, unroll=True)
    return total


def force_pass(qm_all, effective, mm_pos, scale):
    chunks = qm_all.shape[1] // CHUNK
    stacked = jnp.concatenate([qm_all, effective[None, :]], axis=0)
    stacked = jnp.transpose(stacked.reshape(4, chunks, CHUNK), (1, 2, 0))

    def body(running, block):
        d = [block[:, c : c + 1] - mm_pos[c][None, :] for c in range(3)]
        inverse = lax.rsqrt(d[0] * d[0] + d[1] * d[1] + d[2] * d[2] + SOFTEN)
        weight = inverse * inverse * inverse * block[:, 3:4] * scale[None, :]
        return running + jnp.stack([jnp.sum(d[c] * weight, axis=0) for c in range(3)]), None

    total, _ = lax.scan(body, jnp.zeros((3, mm_pos.shape[1]), jnp.float32), stacked, unroll=True)
    return total


def on_device(
    qm_pos,
    species,
    qm_count,
    ghost_owner,
    ghost_slot,
    mm_pos,
    mm_charge,
    species_table,
    potential_gain,
    message_weight,
    hidden_weight,
    energy_readout,
    charge_readout,
):
    rows = qm_pos.shape[1]
    blocks = lax.axis_size("blk")
    me = lax.axis_index("blk")
    kinds = species_table.shape[0]
    coupling = float(mm_pos.shape[1] * blocks * lax.axis_size("rep")) ** (-0.5)

    low_blocks = 1
    while low_blocks * low_blocks < blocks:
        low_blocks *= 2
    own = jnp.concatenate(
        [
            qm_pos,
            species.astype(jnp.float32)[None, :],
            jnp.broadcast_to(qm_count.astype(jnp.float32)[None, :], (1, rows)),
        ],
        axis=0,
    )
    near = gather_doubling(own, "blk", 1, low_blocks)
    mm_some = gather_doubling(
        jnp.concatenate([mm_pos, mm_charge[None, :]], axis=0), "blk", low_blocks, blocks
    )
    partial = potential_pass(near[:3], mm_some)
    total = sum_butterfly(sum_butterfly(partial, "rep"), "blk", low_blocks)
    pull = lax.dynamic_slice_in_dim(total[1:4], (me % low_blocks) * rows, rows, axis=1)
    known = gather_doubling(
        jnp.concatenate([total[0:1] * coupling, near], axis=0), "blk", low_blocks, blocks
    )
    ghost = ghost_owner * rows + ghost_slot
    columns = jnp.arange(blocks * rows)[None, :]
    links = jnp.zeros((rows, blocks * rows), jnp.bfloat16)
    for k in range(ghost.shape[1]):
        links = links + (ghost[:, k : k + 1] == columns).astype(jnp.bfloat16)
    finite = near[0:1, 0:1] == near[0:1, 0:1]
    weights = [species_table.T, message_weight, potential_gain, energy_readout, charge_readout]
    weights = [jnp.where(finite.reshape((1,) * w.ndim), w, jnp.zeros_like(w)) for w in weights]
    known, links, weights = lax.optimization_barrier((known, links, weights))
    table_t, message_weight, potential_gain, energy_readout, charge_readout = weights
    potential_all = known[0]
    qm_all = known[1:4]
    atoms = qm_all.shape[1]
    species_all = known[4].astype(jnp.int32)
    live_all = ((jnp.arange(atoms) % rows).astype(jnp.float32) < known[5]).astype(jnp.float32)

    live = lax.dynamic_slice_in_dim(live_all, me * rows, rows)
    potential = lax.dynamic_slice_in_dim(potential_all, me * rows, rows)
    picks_t = (jnp.arange(kinds)[:, None] == species_all[None, :]).astype(jnp.bfloat16)
    base_t = jnp.dot(table_t, picks_t, preferred_element_type=jnp.float32)
    start_t = (
        live_all[None, :] * (base_t + potential_gain[:, None] * potential_all[None, :])
    ).astype(jnp.bfloat16)
    start = lax.dynamic_slice_in_dim(start_t, me * rows, rows, axis=1).T

    neighbour = lax.dot_general(
        links, start_t, (((1,), (1,)), ((), ())), preferred_element_type=jnp.float32
    ).astype(jnp.bfloat16)

    mixed = start.astype(jnp.float32) + jnp.dot(
        neighbour, message_weight, preferred_element_type=jnp.float32
    )
    before = jnp.dot(mixed.astype(jnp.bfloat16), hidden_weight, preferred_element_type=jnp.float32)
    sigma = jax.nn.sigmoid(before)
    active = before * sigma
    energy_part = live * jnp.sum(active * energy_readout[None, :], axis=1)
    charge_part = live * jnp.sum(active * charge_readout[None, :], axis=1)
    atom_energy = energy_part + charge_part * potential
    back_active = live[:, None] * (
        energy_readout[None, :] + potential[:, None] * charge_readout[None, :]
    )
    back_before = (back_active * sigma * (1.0 + before * (1.0 - sigma))).astype(jnp.bfloat16)
    back_mixed = jnp.dot(back_before, hidden_weight.T, preferred_element_type=jnp.float32)
    back_sum = jnp.dot(
        back_mixed.astype(jnp.bfloat16), message_weight.T, preferred_element_type=jnp.float32
    ).astype(jnp.bfloat16)

    sent = jnp.sum(back_sum.astype(jnp.float32) * potential_gain[None, :], axis=1)
    spread = jnp.sum(links.astype(jnp.float32) * sent[:, None], axis=0) * live_all
    local = charge_part + live * jnp.sum(back_mixed * potential_gain[None, :], axis=1)
    placed = (jnp.arange(atoms) // rows == me).astype(jnp.float32)
    local_all = jnp.tile(local, atoms // rows) * placed
    part = sum_butterfly(spread + local_all, "blk", blocks // 2)
    other = lax.ppermute(part, "blk", [(i, i ^ (blocks // 2)) for i in range(blocks)])
    effective_all = part + other
    effective = lax.dynamic_slice_in_dim(part, me * rows, rows) + lax.dynamic_slice_in_dim(
        other, me * rows, rows
    )
    qm_force = pull * (effective * coupling)[None, :]
    mm_force = force_pass(qm_all, effective_all, mm_pos, -coupling * mm_charge)
    return (atom_energy, qm_force, mm_force)


def solution(mesh):
    placed = (
        P(None, "blk"),
        P("blk"),
        P("blk"),
        P("blk", None),
        P("blk", None),
        P(None, ("blk", "rep")),
        P(("blk", "rep")),
        P(),
        P(),
        P(),
        P(),
        P(),
        P(),
    )
    return jax.shard_map(
        on_device,
        mesh=mesh,
        in_specs=placed,
        out_specs=(P("blk"), P(None, "blk"), P(None, ("blk", "rep"))),
        check_vma=False,
    )
```

```python
import jax
import jax.numpy as jnp
from jax import lax
from jax.sharding import PartitionSpec as P

SOFTEN = 0.25
CHUNK = 512


def gather_doubling(x, axis, first=1, last=None):
    n = lax.axis_size(axis)
    last = n if last is None else last
    me = lax.axis_index(axis)
    step = first
    while step < last:
        other = lax.ppermute(x, axis, [(i, i ^ step) for i in range(n)])
        low = (me // step) % 2 == 0
        x = jnp.where(low, jnp.concatenate([x, other], -1), jnp.concatenate([other, x], -1))
        step *= 2
    return x


def sum_butterfly(x, axis, last=None):
    n = lax.axis_size(axis)
    last = n if last is None else last
    step = 1
    while step < last:
        x = x + lax.ppermute(x, axis, [(i, i ^ step) for i in range(n)])
        step *= 2
    return x


def potential_pass(qm_some, mm_some):
    chunks = mm_some.shape[1] // CHUNK
    cols = [qm_some[c][None, :] for c in range(3)]

    def body(running, block):
        d = [cols[c] - block[:, c : c + 1] for c in range(3)]
        inverse = lax.rsqrt(d[0] * d[0] + d[1] * d[1] + d[2] * d[2] + SOFTEN)
        weighted = inverse * block[:, 3:4]
        cubed = weighted * inverse * inverse
        part = jnp.stack(
            [jnp.sum(weighted, axis=0)] + [jnp.sum(d[c] * cubed, axis=0) for c in range(3)]
        )
        return running + part, None

    stacked = jnp.transpose(mm_some.reshape(4, chunks, CHUNK), (1, 2, 0))
    total, _ = lax.scan(body, jnp.zeros((4, qm_some.shape[1]), jnp.float32), stacked)
    return total


def force_pass(qm_all, effective, mm_pos, scale):
    chunks = qm_all.shape[1] // CHUNK
    stacked = jnp.concatenate([qm_all, effective[None, :]], axis=0)
    stacked = jnp.transpose(stacked.reshape(4, chunks, CHUNK), (1, 2, 0))

    def body(running, block):
        d = [block[:, c : c + 1] - mm_pos[c][None, :] for c in range(3)]
        inverse = lax.rsqrt(d[0] * d[0] + d[1] * d[1] + d[2] * d[2] + SOFTEN)
        weight = inverse * inverse * inverse * block[:, 3:4] * scale[None, :]
        return running + jnp.stack([jnp.sum(d[c] * weight, axis=0) for c in range(3)]), None

    total, _ = lax.scan(body, jnp.zeros((3, mm_pos.shape[1]), jnp.float32), stacked)
    return total


def on_device(
    qm_pos,
    species,
    qm_count,
    ghost_owner,
    ghost_slot,
    mm_pos,
    mm_charge,
    species_table,
    potential_gain,
    message_weight,
    hidden_weight,
    energy_readout,
    charge_readout,
):
    rows = qm_pos.shape[1]
    blocks = lax.axis_size("blk")
    me = lax.axis_index("blk")
    kinds = species_table.shape[0]
    coupling = float(mm_pos.shape[1] * blocks * lax.axis_size("rep")) ** (-0.5)

    low_blocks = 1
    while low_blocks * low_blocks < blocks:
        low_blocks *= 2
    own = jnp.concatenate(
        [
            qm_pos,
            species.astype(jnp.float32)[None, :],
            jnp.broadcast_to(qm_count.astype(jnp.float32)[None, :], (1, rows)),
        ],
        axis=0,
    )
    near = gather_doubling(own, "blk", 1, low_blocks)
    mm_some = jnp.concatenate([mm_pos, mm_charge[None, :]], axis=0)
    step = low_blocks
    while step < blocks // 2:
        mm_some = jnp.concatenate(
            [mm_some, lax.ppermute(mm_some, "blk", [(i, i ^ step) for i in range(blocks)])], -1
        )
        step *= 2
    arriving = lax.ppermute(mm_some, "blk", [(i, i ^ step) for i in range(blocks)])
    partial = potential_pass(near[:3], mm_some) + potential_pass(near[:3], arriving)
    total = sum_butterfly(sum_butterfly(partial, "rep"), "blk", low_blocks)
    pull = lax.dynamic_slice_in_dim(total[1:4], (me % low_blocks) * rows, rows, axis=1)
    known = gather_doubling(
        jnp.concatenate([total[0:1] * coupling, near], axis=0), "blk", low_blocks, blocks
    )
    ghost = ghost_owner * rows + ghost_slot
    columns = jnp.arange(blocks * rows)[None, :]
    links = jnp.zeros((rows, blocks * rows), jnp.bfloat16)
    for k in range(ghost.shape[1]):
        links = links + (ghost[:, k : k + 1] == columns).astype(jnp.bfloat16)
    finite = near[0:1, 0:1] == near[0:1, 0:1]
    weights = [species_table.T, message_weight, potential_gain, energy_readout, charge_readout]
    weights = [jnp.where(finite.reshape((1,) * w.ndim), w, jnp.zeros_like(w)) for w in weights]
    known, links, weights = lax.optimization_barrier((known, links, weights))
    table_t, message_weight, potential_gain, energy_readout, charge_readout = weights
    potential_all = known[0]
    qm_all = known[1:4]
    atoms = qm_all.shape[1]
    species_all = known[4].astype(jnp.int32)
    live_all = ((jnp.arange(atoms) % rows).astype(jnp.float32) < known[5]).astype(jnp.float32)

    live = lax.dynamic_slice_in_dim(live_all, me * rows, rows)
    potential = lax.dynamic_slice_in_dim(potential_all, me * rows, rows)
    picks_t = (jnp.arange(kinds)[:, None] == species_all[None, :]).astype(jnp.bfloat16)
    base_t = jnp.dot(table_t, picks_t, preferred_element_type=jnp.float32)
    start_t = (
        live_all[None, :] * (base_t + potential_gain[:, None] * potential_all[None, :])
    ).astype(jnp.bfloat16)
    start = lax.dynamic_slice_in_dim(start_t, me * rows, rows, axis=1).T

    neighbour = lax.dot_general(
        links, start_t, (((1,), (1,)), ((), ())), preferred_element_type=jnp.float32
    ).astype(jnp.bfloat16)

    mixed = start.astype(jnp.float32) + jnp.dot(
        neighbour, message_weight, preferred_element_type=jnp.float32
    )
    before = jnp.dot(mixed.astype(jnp.bfloat16), hidden_weight, preferred_element_type=jnp.float32)
    sigma = jax.nn.sigmoid(before)
    active = before * sigma
    energy_part = live * jnp.sum(active * energy_readout[None, :], axis=1)
    charge_part = live * jnp.sum(active * charge_readout[None, :], axis=1)
    atom_energy = energy_part + charge_part * potential
    back_active = live[:, None] * (
        energy_readout[None, :] + potential[:, None] * charge_readout[None, :]
    )
    back_before = (back_active * sigma * (1.0 + before * (1.0 - sigma))).astype(jnp.bfloat16)
    back_mixed = jnp.dot(back_before, hidden_weight.T, preferred_element_type=jnp.float32)
    back_sum = jnp.dot(
        back_mixed.astype(jnp.bfloat16), message_weight.T, preferred_element_type=jnp.float32
    ).astype(jnp.bfloat16)

    sent = jnp.sum(back_sum.astype(jnp.float32) * potential_gain[None, :], axis=1)
    spread = jnp.sum(links.astype(jnp.float32) * sent[:, None], axis=0) * live_all
    local = charge_part + live * jnp.sum(back_mixed * potential_gain[None, :], axis=1)
    placed = (jnp.arange(atoms) // rows == me).astype(jnp.float32)
    local_all = jnp.tile(local, atoms // rows) * placed
    part = sum_butterfly(spread + local_all, "blk", blocks // 2)
    other = lax.ppermute(part, "blk", [(i, i ^ (blocks // 2)) for i in range(blocks)])
    effective_all = part + other
    effective = lax.dynamic_slice_in_dim(part, me * rows, rows) + lax.dynamic_slice_in_dim(
        other, me * rows, rows
    )
    qm_force = pull * (effective * coupling)[None, :]
    mm_force = force_pass(qm_all, effective_all, mm_pos, -coupling * mm_charge)
    return (atom_energy, qm_force, mm_force)


def solution(mesh):
    placed = (
        P(None, "blk"),
        P("blk"),
        P("blk"),
        P("blk", None),
        P("blk", None),
        P(None, ("blk", "rep")),
        P(("blk", "rep")),
        P(),
        P(),
        P(),
        P(),
        P(),
        P(),
    )
    return jax.shard_map(
        on_device,
        mesh=mesh,
        in_specs=placed,
        out_specs=(P("blk"), P(None, "blk"), P(None, ("blk", "rep"))),
        check_vma=False,
    )
```

```python
import jax
import jax.numpy as jnp
from jax import lax
from jax.sharding import PartitionSpec as P

SOFTEN = 0.25
CHUNK = 512


def gather_doubling(x, axis, first=1, last=None):
    n = lax.axis_size(axis)
    last = n if last is None else last
    me = lax.axis_index(axis)
    step = first
    while step < last:
        other = lax.ppermute(x, axis, [(i, i ^ step) for i in range(n)])
        low = (me // step) % 2 == 0
        x = jnp.where(low, jnp.concatenate([x, other], -1), jnp.concatenate([other, x], -1))
        step *= 2
    return x


def sum_butterfly(x, axis, last=None):
    n = lax.axis_size(axis)
    last = n if last is None else last
    step = 1
    while step < last:
        x = x + lax.ppermute(x, axis, [(i, i ^ step) for i in range(n)])
        step *= 2
    return x


def potential_pass(qm_some, mm_some):
    cols = [qm_some[c][None, :] for c in range(3)]
    total = jnp.zeros((4, qm_some.shape[1]), jnp.float32)
    for lo in range(0, mm_some.shape[1], CHUNK):
        block = mm_some[:, lo : lo + CHUNK].T
        d = [cols[c] - block[:, c : c + 1] for c in range(3)]
        inverse = lax.rsqrt(d[0] * d[0] + d[1] * d[1] + d[2] * d[2] + SOFTEN)
        weighted = inverse * block[:, 3:4]
        cubed = weighted * inverse * inverse
        total = total + jnp.stack(
            [jnp.sum(weighted, axis=0)] + [jnp.sum(d[c] * cubed, axis=0) for c in range(3)]
        )
    return total


def force_pass(qm_all, effective, mm_pos, scale):
    chunks = qm_all.shape[1] // CHUNK
    stacked = jnp.concatenate([qm_all, effective[None, :]], axis=0)
    stacked = jnp.transpose(stacked.reshape(4, chunks, CHUNK), (1, 2, 0))

    def body(running, block):
        d = [block[:, c : c + 1] - mm_pos[c][None, :] for c in range(3)]
        inverse = lax.rsqrt(d[0] * d[0] + d[1] * d[1] + d[2] * d[2] + SOFTEN)
        weight = inverse * inverse * inverse * block[:, 3:4] * scale[None, :]
        return running + jnp.stack([jnp.sum(d[c] * weight, axis=0) for c in range(3)]), None

    total, _ = lax.scan(body, jnp.zeros((3, mm_pos.shape[1]), jnp.float32), stacked)
    return total


def on_device(
    qm_pos,
    species,
    qm_count,
    ghost_owner,
    ghost_slot,
    mm_pos,
    mm_charge,
    species_table,
    potential_gain,
    message_weight,
    hidden_weight,
    energy_readout,
    charge_readout,
):
    rows = qm_pos.shape[1]
    blocks = lax.axis_size("blk")
    me = lax.axis_index("blk")
    kinds = species_table.shape[0]
    coupling = float(mm_pos.shape[1] * blocks * lax.axis_size("rep")) ** (-0.5)

    low_blocks = 1
    while low_blocks * low_blocks < blocks:
        low_blocks *= 2
    own = jnp.concatenate(
        [
            qm_pos,
            species.astype(jnp.float32)[None, :],
            jnp.broadcast_to(qm_count.astype(jnp.float32)[None, :], (1, rows)),
        ],
        axis=0,
    )
    near = gather_doubling(own, "blk", 1, low_blocks)
    mm_some = jnp.concatenate([mm_pos, mm_charge[None, :]], axis=0)
    step = low_blocks
    while step < blocks // 2:
        mm_some = jnp.concatenate(
            [mm_some, lax.ppermute(mm_some, "blk", [(i, i ^ step) for i in range(blocks)])], -1
        )
        step *= 2
    arriving = lax.ppermute(mm_some, "blk", [(i, i ^ step) for i in range(blocks)])
    partial = potential_pass(near[:3], mm_some) + potential_pass(near[:3], arriving)
    total = sum_butterfly(sum_butterfly(partial, "rep"), "blk", low_blocks)
    pull = lax.dynamic_slice_in_dim(total[1:4], (me % low_blocks) * rows, rows, axis=1)
    known = gather_doubling(
        jnp.concatenate([total[0:1] * coupling, near], axis=0), "blk", low_blocks, blocks
    )
    ghost = ghost_owner * rows + ghost_slot
    columns = jnp.arange(blocks * rows)[None, :]
    links = jnp.zeros((rows, blocks * rows), jnp.bfloat16)
    for k in range(ghost.shape[1]):
        links = links + (ghost[:, k : k + 1] == columns).astype(jnp.bfloat16)
    finite = near[0:1, 0:1] == near[0:1, 0:1]
    weights = [species_table.T, message_weight, potential_gain, energy_readout, charge_readout]
    weights = [jnp.where(finite.reshape((1,) * w.ndim), w, jnp.zeros_like(w)) for w in weights]
    known, links, weights = lax.optimization_barrier((known, links, weights))
    table_t, message_weight, potential_gain, energy_readout, charge_readout = weights
    potential_all = known[0]
    qm_all = known[1:4]
    atoms = qm_all.shape[1]
    species_all = known[4].astype(jnp.int32)
    live_all = ((jnp.arange(atoms) % rows).astype(jnp.float32) < known[5]).astype(jnp.float32)

    live = lax.dynamic_slice_in_dim(live_all, me * rows, rows)
    potential = lax.dynamic_slice_in_dim(potential_all, me * rows, rows)
    picks_t = (jnp.arange(kinds)[:, None] == species_all[None, :]).astype(jnp.bfloat16)
    base_t = jnp.dot(table_t, picks_t, preferred_element_type=jnp.float32)
    start_t = (
        live_all[None, :] * (base_t + potential_gain[:, None] * potential_all[None, :])
    ).astype(jnp.bfloat16)
    start = lax.dynamic_slice_in_dim(start_t, me * rows, rows, axis=1).T

    neighbour = lax.dot_general(
        links, start_t, (((1,), (1,)), ((), ())), preferred_element_type=jnp.float32
    ).astype(jnp.bfloat16)

    mixed = start.astype(jnp.float32) + jnp.dot(
        neighbour, message_weight, preferred_element_type=jnp.float32
    )
    before = jnp.dot(mixed.astype(jnp.bfloat16), hidden_weight, preferred_element_type=jnp.float32)
    sigma = jax.nn.sigmoid(before)
    active = before * sigma
    energy_part = live * jnp.sum(active * energy_readout[None, :], axis=1)
    charge_part = live * jnp.sum(active * charge_readout[None, :], axis=1)
    atom_energy = energy_part + charge_part * potential
    back_active = live[:, None] * (
        energy_readout[None, :] + potential[:, None] * charge_readout[None, :]
    )
    back_before = (back_active * sigma * (1.0 + before * (1.0 - sigma))).astype(jnp.bfloat16)
    back_mixed = jnp.dot(back_before, hidden_weight.T, preferred_element_type=jnp.float32)
    back_sum = jnp.dot(
        back_mixed.astype(jnp.bfloat16), message_weight.T, preferred_element_type=jnp.float32
    ).astype(jnp.bfloat16)

    sent = jnp.sum(back_sum.astype(jnp.float32) * potential_gain[None, :], axis=1)
    spread = jnp.sum(links.astype(jnp.float32) * sent[:, None], axis=0) * live_all
    local = charge_part + live * jnp.sum(back_mixed * potential_gain[None, :], axis=1)
    placed = (jnp.arange(atoms) // rows == me).astype(jnp.float32)
    local_all = jnp.tile(local, atoms // rows) * placed
    part = sum_butterfly(spread + local_all, "blk", blocks // 2)
    other = lax.ppermute(part, "blk", [(i, i ^ (blocks // 2)) for i in range(blocks)])
    effective_all = part + other
    effective = lax.dynamic_slice_in_dim(part, me * rows, rows) + lax.dynamic_slice_in_dim(
        other, me * rows, rows
    )
    qm_force = pull * (effective * coupling)[None, :]
    mm_force = force_pass(qm_all, effective_all, mm_pos, -coupling * mm_charge)
    return (atom_energy, qm_force, mm_force)


def solution(mesh):
    placed = (
        P(None, "blk"),
        P("blk"),
        P("blk"),
        P("blk", None),
        P("blk", None),
        P(None, ("blk", "rep")),
        P(("blk", "rep")),
        P(),
        P(),
        P(),
        P(),
        P(),
        P(),
    )
    return jax.shard_map(
        on_device,
        mesh=mesh,
        in_specs=placed,
        out_specs=(P("blk"), P(None, "blk"), P(None, ("blk", "rep"))),
        check_vma=False,
    )
```

```python
import jax
import jax.numpy as jnp
from jax import lax
from jax.sharding import PartitionSpec as P

SOFTEN = 0.25
CHUNK = 512


def gather_doubling(x, axis, first=1, last=None):
    n = lax.axis_size(axis)
    last = n if last is None else last
    me = lax.axis_index(axis)
    step = first
    while step < last:
        other = lax.ppermute(x, axis, [(i, i ^ step) for i in range(n)])
        low = (me // step) % 2 == 0
        x = jnp.where(low, jnp.concatenate([x, other], -1), jnp.concatenate([other, x], -1))
        step *= 2
    return x


def sum_butterfly(x, axis, last=None):
    n = lax.axis_size(axis)
    last = n if last is None else last
    step = 1
    while step < last:
        x = x + lax.ppermute(x, axis, [(i, i ^ step) for i in range(n)])
        step *= 2
    return x


def potential_pass(qm_some, mm_some):
    chunks = mm_some.shape[1] // CHUNK
    cols = [qm_some[c][None, :] for c in range(3)]

    def body(running, block):
        d = [cols[c] - block[:, c : c + 1] for c in range(3)]
        inverse = lax.rsqrt(d[0] * d[0] + d[1] * d[1] + d[2] * d[2] + SOFTEN)
        weighted = inverse * block[:, 3:4]
        cubed = weighted * inverse * inverse
        part = jnp.stack(
            [jnp.sum(weighted, axis=0)] + [jnp.sum(d[c] * cubed, axis=0) for c in range(3)]
        )
        return running + part, None

    stacked = jnp.transpose(mm_some.reshape(4, chunks, CHUNK), (1, 2, 0))
    total, _ = lax.scan(body, jnp.zeros((4, qm_some.shape[1]), jnp.float32), stacked)
    return total


def force_pass(qm_all, effective, mm_pos, scale):
    chunks = qm_all.shape[1] // CHUNK
    stacked = jnp.concatenate([qm_all, effective[None, :]], axis=0)
    stacked = jnp.transpose(stacked.reshape(4, chunks, CHUNK), (1, 2, 0))

    def body(running, block):
        d = [block[:, c : c + 1] - mm_pos[c][None, :] for c in range(3)]
        inverse = lax.rsqrt(d[0] * d[0] + d[1] * d[1] + d[2] * d[2] + SOFTEN)
        weight = inverse * inverse * inverse * block[:, 3:4] * scale[None, :]
        return running + jnp.stack([jnp.sum(d[c] * weight, axis=0) for c in range(3)]), None

    total, _ = lax.scan(body, jnp.zeros((3, mm_pos.shape[1]), jnp.float32), stacked)
    return total


def on_device(
    qm_pos,
    species,
    qm_count,
    ghost_owner,
    ghost_slot,
    mm_pos,
    mm_charge,
    species_table,
    potential_gain,
    message_weight,
    hidden_weight,
    energy_readout,
    charge_readout,
):
    rows = qm_pos.shape[1]
    blocks = lax.axis_size("blk")
    me = lax.axis_index("blk")
    kinds = species_table.shape[0]
    coupling = float(mm_pos.shape[1] * blocks * lax.axis_size("rep")) ** (-0.5)

    low_blocks = 1
    while low_blocks * low_blocks < blocks:
        low_blocks *= 2
    own = jnp.concatenate(
        [
            qm_pos,
            species.astype(jnp.float32)[None, :],
            jnp.broadcast_to(qm_count.astype(jnp.float32)[None, :], (1, rows)),
        ],
        axis=0,
    )
    near = gather_doubling(own, "blk", 1, low_blocks)
    mm_some = jnp.concatenate([mm_pos, mm_charge[None, :]], axis=0)
    partial = potential_pass(near[:3], mm_some)
    step = low_blocks
    while step < blocks:
        arriving = lax.ppermute(mm_some, "blk", [(i, i ^ step) for i in range(blocks)])
        partial = partial + potential_pass(near[:3], arriving)
        if step * 2 < blocks:
            mm_some = jnp.concatenate([mm_some, arriving], -1)
        step *= 2
    total = sum_butterfly(sum_butterfly(partial, "rep"), "blk", low_blocks)
    pull = lax.dynamic_slice_in_dim(total[1:4], (me % low_blocks) * rows, rows, axis=1)
    known = gather_doubling(
        jnp.concatenate([total[0:1] * coupling, near], axis=0), "blk", low_blocks, blocks
    )
    ghost = ghost_owner * rows + ghost_slot
    columns = jnp.arange(blocks * rows)[None, :]
    links = jnp.zeros((rows, blocks * rows), jnp.bfloat16)
    for k in range(ghost.shape[1]):
        links = links + (ghost[:, k : k + 1] == columns).astype(jnp.bfloat16)
    finite = near[0:1, 0:1] == near[0:1, 0:1]
    weights = [species_table.T, message_weight, potential_gain, energy_readout, charge_readout]
    weights = [jnp.where(finite.reshape((1,) * w.ndim), w, jnp.zeros_like(w)) for w in weights]
    known, links, weights = lax.optimization_barrier((known, links, weights))
    table_t, message_weight, potential_gain, energy_readout, charge_readout = weights
    potential_all = known[0]
    qm_all = known[1:4]
    atoms = qm_all.shape[1]
    species_all = known[4].astype(jnp.int32)
    live_all = ((jnp.arange(atoms) % rows).astype(jnp.float32) < known[5]).astype(jnp.float32)

    live = lax.dynamic_slice_in_dim(live_all, me * rows, rows)
    potential = lax.dynamic_slice_in_dim(potential_all, me * rows, rows)
    picks_t = (jnp.arange(kinds)[:, None] == species_all[None, :]).astype(jnp.bfloat16)
    base_t = jnp.dot(table_t, picks_t, preferred_element_type=jnp.float32)
    start_t = (
        live_all[None, :] * (base_t + potential_gain[:, None] * potential_all[None, :])
    ).astype(jnp.bfloat16)
    start = lax.dynamic_slice_in_dim(start_t, me * rows, rows, axis=1).T

    neighbour = lax.dot_general(
        links, start_t, (((1,), (1,)), ((), ())), preferred_element_type=jnp.float32
    ).astype(jnp.bfloat16)

    mixed = start.astype(jnp.float32) + jnp.dot(
        neighbour, message_weight, preferred_element_type=jnp.float32
    )
    before = jnp.dot(mixed.astype(jnp.bfloat16), hidden_weight, preferred_element_type=jnp.float32)
    sigma = jax.nn.sigmoid(before)
    active = before * sigma
    energy_part = live * jnp.sum(active * energy_readout[None, :], axis=1)
    charge_part = live * jnp.sum(active * charge_readout[None, :], axis=1)
    atom_energy = energy_part + charge_part * potential
    back_active = live[:, None] * (
        energy_readout[None, :] + potential[:, None] * charge_readout[None, :]
    )
    back_before = (back_active * sigma * (1.0 + before * (1.0 - sigma))).astype(jnp.bfloat16)
    back_mixed = jnp.dot(back_before, hidden_weight.T, preferred_element_type=jnp.float32)
    back_sum = jnp.dot(
        back_mixed.astype(jnp.bfloat16), message_weight.T, preferred_element_type=jnp.float32
    ).astype(jnp.bfloat16)

    sent = jnp.sum(back_sum.astype(jnp.float32) * potential_gain[None, :], axis=1)
    spread = jnp.sum(links.astype(jnp.float32) * sent[:, None], axis=0) * live_all
    local = charge_part + live * jnp.sum(back_mixed * potential_gain[None, :], axis=1)
    placed = (jnp.arange(atoms) // rows == me).astype(jnp.float32)
    local_all = jnp.tile(local, atoms // rows) * placed
    part = sum_butterfly(spread + local_all, "blk", blocks // 2)
    other = lax.ppermute(part, "blk", [(i, i ^ (blocks // 2)) for i in range(blocks)])
    effective_all = part + other
    effective = lax.dynamic_slice_in_dim(part, me * rows, rows) + lax.dynamic_slice_in_dim(
        other, me * rows, rows
    )
    qm_force = pull * (effective * coupling)[None, :]
    mm_force = force_pass(qm_all, effective_all, mm_pos, -coupling * mm_charge)
    return (atom_energy, qm_force, mm_force)


def solution(mesh):
    placed = (
        P(None, "blk"),
        P("blk"),
        P("blk"),
        P("blk", None),
        P("blk", None),
        P(None, ("blk", "rep")),
        P(("blk", "rep")),
        P(),
        P(),
        P(),
        P(),
        P(),
        P(),
    )
    return jax.shard_map(
        on_device,
        mesh=mesh,
        in_specs=placed,
        out_specs=(P("blk"), P(None, "blk"), P(None, ("blk", "rep"))),
        check_vma=False,
    )
```
